512 devices in a mesh: seq: 32 (over z, core), dp: 4 (over x), tensor: 4 (over y).
Axes of the slice: x: 4, y: 4, z: 16, core: 2. Of those that a mesh axis runs over, the one named last changes fastest.
Arguments:
- attention_queries: bfloat16 [4, 4096, 3584], P('dp', 'seq', 'tensor')
- attention_keys: bfloat16 [4, 4096, 512], P('dp', 'seq', 'tensor')
- attention_values: bfloat16 [4, 4096, 512], P('dp', 'seq', 'tensor')
- key_window_length: int32 [4], P('tensor'), may hold values from 128 to 512, as said below
- norm_gain: float32 [3584], P('tensor'), may hold values from 0.5 to 2
- spike_levels: int32 [3584], P('tensor'), may hold values from 1 to 4
- lin_queries: bfloat16 [4, 4096, 3584], P('dp', 'seq', 'tensor'), may hold values from -6 to 6
- lin_keys: bfloat16 [4, 4096, 3584], P('dp', 'seq', 'tensor'), may hold values from -6 to 6
- decay_logs: float32 [4, 28, 4096], P('dp', 'tensor', 'seq'), as said below
- cotangent: bfloat16 [4, 4096, 3584], P('dp', 'seq', 'tensor')
Outputs:
- layer_output: bfloat16 [4, 4096, 3584], P('dp', 'seq', 'tensor')
- query_grads: bfloat16 [4, 4096, 3584], P('dp', 'seq', 'tensor')
- key_gradient: bfloat16 [4, 4096, 512], P('dp', 'seq', 'tensor')
- value_gradient: bfloat16 [4, 4096, 512], P('dp', 'seq', 'tensor')
- gain_grads: float32 [3584], P('tensor')
The draws below stay inside these ranges and needn't reach their ends.
Inputs may be any that keep to these rules, and one draw needn't show every extreme that they name: Key head g lets query t see positions j with t - key_window_length[g] < j <= t; some head has exactly 512. `decay_logs`: non-positive.
All inputs are finite; a program needn't handle non-finite values.
Results may differ from the reference program's by a relative error of at most 0.015.
Values may be sent and summed in bfloat16 or wider, within the bound.
No kernel may reach another device: no remote copies, remote signals or barrier semaphores. Data moves between devices by JAX's collectives and lax.ppermute only.
A program may use at most 128 MiB of HBM per device.

```python
import math
import jax
import jax.numpy as jnp
from jax import lax

TEST_LANES = 28
KEY_VALUE_HEADS = 4
HEAD_SIZE = 128
D = 3584
LONGEST_WINDOW = 512
SEQUENCE_SHARD = 128
LENGTH = 4096
BATCH = 4
N_SEQ = 32
N_DP = 4


def attention_draw(key):
    base_offset = jax.random.fold_in(key, 7)
    key_query, random_keys_split = jax.random.split(base_offset, 2)
    batch_count = N_DP
    whole_span = SEQUENCE_SHARD * N_SEQ
    query_block = jax.random.normal(key_query, (batch_count, whole_span, TEST_LANES, HEAD_SIZE), jnp.float32)
    key_row_block = jax.random.normal(random_keys_split, (batch_count, whole_span, KEY_VALUE_HEADS, HEAD_SIZE), jnp.float32)
    return (query_block, key_row_block)


def draw_attention_queries(key, part):
    query_block, key_row_block = attention_draw(key)
    return query_block.reshape(N_DP, SEQUENCE_SHARD * N_SEQ, TEST_LANES * HEAD_SIZE).astype(jnp.bfloat16)


def draw_attention_keys(key, part):
    query_block, key_row_block = attention_draw(key)
    return key_row_block.reshape(N_DP, SEQUENCE_SHARD * N_SEQ, KEY_VALUE_HEADS * HEAD_SIZE).astype(jnp.bfloat16)


def draw_attention_values(key, part):
    whole_span = SEQUENCE_SHARD * N_SEQ
    random_main_key = jax.random.fold_in(jax.random.fold_in(key, 3), 0)
    scale_factors = 3.0 ** (jnp.arange(KEY_VALUE_HEADS, dtype=jnp.float32) / max(KEY_VALUE_HEADS - 1, 1))
    base_offset = jax.random.normal(random_main_key, (N_DP, whole_span, KEY_VALUE_HEADS, HEAD_SIZE), jnp.float32)
    return (base_offset * scale_factors[:, None]).reshape(N_DP, whole_span, KEY_VALUE_HEADS * HEAD_SIZE).astype(jnp.bfloat16)


def draw_key_window_length(key, part):
    random_draw_key, random_pick_key = jax.random.split(jax.random.fold_in(key, 5))
    drawn_sample = jax.random.randint(random_draw_key, (KEY_VALUE_HEADS,), LONGEST_WINDOW // 4, LONGEST_WINDOW + 1)
    chosen_heads = jax.random.randint(random_pick_key, (), 0, KEY_VALUE_HEADS)
    return drawn_sample.at[chosen_heads].set(LONGEST_WINDOW)


def draw_decay_logs(key, part):
    whole_span = SEQUENCE_SHARD * N_SEQ
    divided_slices = jax.random.split(jax.random.fold_in(key, 9), 6)
    fast_odds = 2
    quick_pointer = jax.random.randint(divided_slices[0], (N_DP, TEST_LANES, 1), 0, fast_odds) == 0
    lookback_span = jax.random.uniform(divided_slices[1], (N_DP, TEST_LANES, 1), jnp.float32, 30.0, 50.0)
    gentle_pointer = jax.random.uniform(divided_slices[2], (N_DP, TEST_LANES, 1), jnp.float32, 0.1, 0.5) / whole_span
    coarse_estimate = jnp.exp(jax.random.uniform(divided_slices[3], (N_DP, TEST_LANES, whole_span), jnp.float32, -0.7, 0.7))
    pulse_ratios = jnp.where(quick_pointer, 1.0 / lookback_span, gentle_pointer) * coarse_estimate
    pulse_occasions = jax.random.randint(divided_slices[4], (N_DP, TEST_LANES, 2), 0, whole_span)
    thrown_items = jnp.log(jax.random.uniform(divided_slices[5], (N_DP, TEST_LANES, 2), jnp.float32, 0.5, 0.8))
    symbol_place = jnp.arange(N_DP)[:, None, None]
    lane_ordinal = jnp.arange(TEST_LANES)[None, :, None]
    return (-pulse_ratios).at[symbol_place, lane_ordinal, pulse_occasions].add(thrown_items)


def draw_cotangent(key, part):
    whole_span = SEQUENCE_SHARD * N_SEQ
    random_main_key = jax.random.fold_in(key, 13)
    position = jnp.arange(whole_span, dtype=jnp.float32) / max(whole_span - 1, 1)
    sequence = jnp.arange(N_DP, dtype=jnp.float32) / max(N_DP - 1, 1)
    scale_factors = (1.0 + 2.0 * position)[None, :, None] * (1.0 + sequence)[:, None, None]
    base_offset = jax.random.normal(random_main_key, (N_DP, whole_span, TEST_LANES * HEAD_SIZE), jnp.float32)
    return (base_offset * scale_factors).astype(jnp.bfloat16)


def with_ends(array, stream_key, least, high):
    index_at = [jax.random.randint(jax.random.fold_in(stream_key, axis), (), 0, length) for axis, length in enumerate(array.shape)]
    longest = array.shape.index(max(array.shape))
    next_to = index_at[:longest] + [(index_at[longest] + 1) % array.shape[longest]] + index_at[longest + 1:]
    return array.at[tuple(index_at)].set(least).at[tuple(next_to)].set(high)


def shard_levels(stream_key, dims, pieces, smallest, largest):
    def one(axis_at, blocks):
        steps = jax.random.uniform(jax.random.fold_in(jax.random.fold_in(stream_key, 6), axis_at), (blocks,), jnp.float32, smallest / len(pieces), largest / len(pieces))
        return jnp.repeat(jnp.exp(steps), dims[axis_at] // blocks).reshape((-1,) + (1,) * (len(dims) - axis_at - 1))

    gain = one(*pieces[0])
    for cut in pieces[1:]:
        gain = gain * one(*cut)
    return gain


def gaussian(rng, shape, deviation, reach, pieces=(), held_as=jnp.bfloat16):
    drawn = deviation * jax.random.normal(rng, shape, jnp.float32)
    if pieces:
        drawn = drawn * shard_levels(rng, shape, pieces, -0.22, 0.18)
    return jnp.clip(drawn, -reach, reach).astype(held_as)


def setup_inputs(seed: int = 0) -> dict:
    splits = jax.random.split(jax.random.key(seed), 11)
    return {
        "attention_queries": draw_attention_queries(jax.random.fold_in(splits[10], 71), 0),
        "attention_keys": draw_attention_keys(jax.random.fold_in(splits[10], 71), 0),
        "attention_values": draw_attention_values(jax.random.fold_in(splits[10], 71), 0),
        "key_window_length": draw_key_window_length(jax.random.fold_in(splits[10], 71), 0),
        "norm_gain": jnp.clip(jnp.exp(math.log(2.0) - 1.3862944 * jax.random.uniform(splits[4], (D,), jnp.float32) ** shard_levels(splits[4], (D,), ((0, 4),), -0.2, 0.2)), 0.5, 2.0),
        "spike_levels": with_ends(jax.random.randint(splits[5], (D,), 1, 5), jax.random.fold_in(splits[5], 1), 1, 4).astype(jnp.int32),
        "lin_queries": gaussian(splits[6], (BATCH, LENGTH, D), 1.0, 6.0, ((0, 4), (1, 32), (2, 4))),
        "lin_keys": gaussian(splits[7], (BATCH, LENGTH, D), 1.0, 6.0, ((0, 4), (1, 32), (2, 4))),
        "decay_logs": draw_decay_logs(jax.random.fold_in(splits[10], 71), 0),
        "cotangent": draw_cotangent(jax.random.fold_in(splits[10], 71), 0),
    }


precise = lax.Precision.HIGHEST
epsilon = 1e-06

def masked_logits(query_block, key_row_block, first_query, key_reach):
    block_rows = query_block.shape[1]
    key_span = key_row_block.shape[0] - block_rows
    scaling = 1.0 / math.sqrt(query_block.shape[2])
    logits = jnp.einsum('gsd,kd->gsk', query_block.astype(jnp.float32), key_row_block.astype(jnp.float32)) * scaling
    query_pos = first_query + jnp.arange(block_rows, dtype=jnp.int32)[:, None]
    key_pos = first_query - key_span + jnp.arange(key_row_block.shape[0], dtype=jnp.int32)[None, :]
    allowed = (key_pos >= 0) & (key_pos <= query_pos) & (key_pos > query_pos - key_reach)
    return (jnp.where(allowed[None], logits, -jnp.inf), scaling)

def padded_window(group_keys):
    key_span = (LONGEST_WINDOW + SEQUENCE_SHARD - 1) // SEQUENCE_SHARD * SEQUENCE_SHARD
    padding = jnp.zeros((key_span, group_keys.shape[1]), group_keys.dtype)
    return (jnp.concatenate([padding, group_keys], axis=0), key_span)

def attend_forward(group_queries, group_keys, group_values, key_reach):
    whole_span = group_keys.shape[0]
    padded_keys, key_span = padded_window(group_keys)
    padded_values, key_span = padded_window(group_values)

    def one_block(block_index):
        first_query = block_index * SEQUENCE_SHARD
        query_block = lax.dynamic_slice_in_dim(group_queries, first_query, SEQUENCE_SHARD, 1)
        key_row_block = lax.dynamic_slice_in_dim(padded_keys, first_query, key_span + SEQUENCE_SHARD, 0)
        value_rows = lax.dynamic_slice_in_dim(padded_values, first_query, key_span + SEQUENCE_SHARD, 0)
        logits, scaling = masked_logits(query_block, key_row_block, first_query, key_reach)
        row_max = lax.optimization_barrier(jnp.max(logits, axis=-1))
        exponent = jnp.exp(logits - row_max[..., None])
        row_sum = lax.optimization_barrier(jnp.sum(exponent, axis=-1))
        weights = (exponent / row_sum[..., None]).astype(jnp.bfloat16)
        output = jnp.einsum('gsk,kd->gsd', weights.astype(jnp.float32), value_rows.astype(jnp.float32))
        return (output.astype(jnp.bfloat16), row_max, row_sum)
    outputs, maxima, sums = lax.map(one_block, jnp.arange(whole_span // SEQUENCE_SHARD, dtype=jnp.int32))
    head_groups = group_queries.shape[0]
    outputs = outputs.transpose(1, 0, 2, 3).reshape(head_groups, whole_span, HEAD_SIZE)
    maxima = maxima.transpose(1, 0, 2).reshape(head_groups, whole_span)
    sums = sums.transpose(1, 0, 2).reshape(head_groups, whole_span)
    return (outputs, maxima, sums)

def attend_backward(group_queries, group_keys, group_values, group_gradient, maxima, sums, key_reach):
    whole_span = group_keys.shape[0]
    padded_keys, key_span = padded_window(group_keys)
    padded_values, key_span = padded_window(group_values)
    empty = jnp.zeros((key_span + whole_span, HEAD_SIZE), jnp.float32)

    def one_block(carry, block_index):
        key_accumulator, value_accumulator = carry
        first_query = block_index * SEQUENCE_SHARD
        query_block = lax.dynamic_slice_in_dim(group_queries, first_query, SEQUENCE_SHARD, 1)
        grad_rows = lax.dynamic_slice_in_dim(group_gradient, first_query, SEQUENCE_SHARD, 1)
        block_max = lax.dynamic_slice_in_dim(maxima, first_query, SEQUENCE_SHARD, 1)
        block_sum = lax.dynamic_slice_in_dim(sums, first_query, SEQUENCE_SHARD, 1)
        key_row_block = lax.dynamic_slice_in_dim(padded_keys, first_query, key_span + SEQUENCE_SHARD, 0)
        value_rows = lax.dynamic_slice_in_dim(padded_values, first_query, key_span + SEQUENCE_SHARD, 0)
        logits, scaling = masked_logits(query_block, key_row_block, first_query, key_reach)
        probs = jnp.exp(logits - block_max[..., None]) / block_sum[..., None]
        weights = probs.astype(jnp.bfloat16)
        prob_grad = jnp.einsum('gsd,kd->gsk', grad_rows.astype(jnp.float32), value_rows.astype(jnp.float32))
        row_delta = lax.optimization_barrier(jnp.sum(probs * prob_grad, axis=-1, keepdims=True))
        logit_grad = (probs * (prob_grad - row_delta) * scaling).astype(jnp.bfloat16)
        query_grad = jnp.einsum('gsk,kd->gsd', logit_grad.astype(jnp.float32), key_row_block.astype(jnp.float32))
        key_part = jnp.einsum('gsk,gsd->kd', logit_grad.astype(jnp.float32), query_block.astype(jnp.float32))
        value_part = jnp.einsum('gsk,gsd->kd', weights.astype(jnp.float32), grad_rows.astype(jnp.float32))
        old_keys = lax.dynamic_slice_in_dim(key_accumulator, first_query, key_span + SEQUENCE_SHARD, 0)
        old_values = lax.dynamic_slice_in_dim(value_accumulator, first_query, key_span + SEQUENCE_SHARD, 0)
        key_accumulator = lax.dynamic_update_slice_in_dim(key_accumulator, old_keys + key_part, first_query, 0)
        value_accumulator = lax.dynamic_update_slice_in_dim(value_accumulator, old_values + value_part, first_query, 0)
        return ((key_accumulator, value_accumulator), query_grad)
    (key_accumulator, value_accumulator), query_parts = lax.scan(one_block, (empty, empty), jnp.arange(whole_span // SEQUENCE_SHARD, dtype=jnp.int32))
    head_groups = group_queries.shape[0]
    query_parts = query_parts.transpose(1, 0, 2, 3).reshape(head_groups, whole_span, HEAD_SIZE)
    return (query_parts, key_accumulator[key_span:], value_accumulator[key_span:])

def decay_weights(block_queries, block_keys, cumulative):
    block_rows = cumulative.shape[0]
    lower_mask = jnp.arange(block_rows)[:, None] >= jnp.arange(block_rows)[None, :]
    gaps = jnp.where(lower_mask, cumulative[:, None] - cumulative[None, :], 0.0)
    products = jnp.dot(block_queries, block_keys.T, preferred_element_type=jnp.float32)
    return jnp.where(lower_mask, jnp.exp(gaps), 0.0) * products

def membrane_forward(head_queries, head_keys, head_spikes, decay_row):
    count = head_keys.shape[0] // SEQUENCE_SHARD
    stacked = (head_queries.reshape(count, SEQUENCE_SHARD, HEAD_SIZE), head_keys.reshape(count, SEQUENCE_SHARD, HEAD_SIZE), head_spikes.reshape(count, SEQUENCE_SHARD, HEAD_SIZE), decay_row.reshape(count, SEQUENCE_SHARD))

    def one_block(state, divided_slices):
        block_queries, block_keys, block_spikes, block_logs = divided_slices
        cumulative = jnp.cumsum(block_logs)
        decayed = decay_weights(block_queries, block_keys, cumulative)
        spike_float = block_spikes.astype(jnp.float32)
        carried = jnp.dot(block_queries.astype(jnp.float32), state, precision=precise)
        result = jnp.dot(decayed, spike_float, precision=precise) + jnp.exp(cumulative)[:, None] * carried
        weighted = block_keys.astype(jnp.float32) * jnp.exp(cumulative[-1] - cumulative)[:, None]
        state = jnp.exp(cumulative[-1]) * state + jnp.dot(weighted.T, spike_float, precision=precise)
        return (state, result)
    _, results = lax.scan(one_block, jnp.zeros((HEAD_SIZE, HEAD_SIZE), jnp.float32), stacked)
    return results.reshape(count * SEQUENCE_SHARD, HEAD_SIZE)

def membrane_backward(head_queries, head_keys, decay_row, head_grads):
    count = head_keys.shape[0] // SEQUENCE_SHARD
    stacked = (head_queries.reshape(count, SEQUENCE_SHARD, HEAD_SIZE), head_keys.reshape(count, SEQUENCE_SHARD, HEAD_SIZE), decay_row.reshape(count, SEQUENCE_SHARD), head_grads.reshape(count, SEQUENCE_SHARD, HEAD_SIZE))

    def one_block(carry, divided_slices):
        block_queries, block_keys, block_logs, block_grads = divided_slices
        cumulative = jnp.cumsum(block_logs)
        decayed = decay_weights(block_queries, block_keys, cumulative)
        later = jnp.dot(block_keys.astype(jnp.float32), carry, precision=precise)
        result = jnp.dot(decayed.T, block_grads, precision=precise) + jnp.exp(cumulative[-1] - cumulative)[:, None] * later
        weighted = block_queries.astype(jnp.float32) * jnp.exp(cumulative)[:, None]
        carry = jnp.dot(weighted.T, block_grads, precision=precise) + jnp.exp(cumulative[-1]) * carry
        return (carry, result)
    _, results = lax.scan(one_block, jnp.zeros((HEAD_SIZE, HEAD_SIZE), jnp.float32), stacked, reverse=True)
    return results.reshape(count * SEQUENCE_SHARD, HEAD_SIZE)

def reference(attention_queries, attention_keys, attention_values, key_window_length, norm_gain, spike_levels, lin_queries, lin_keys, decay_logs, cotangent):
    batch_count, whole_span, width_all = attention_queries.shape
    head_groups = TEST_LANES // KEY_VALUE_HEADS
    query_block = attention_queries.reshape(batch_count, whole_span, KEY_VALUE_HEADS, head_groups, HEAD_SIZE).transpose(0, 2, 3, 1, 4)
    key_head_rows = attention_keys.reshape(batch_count, whole_span, KEY_VALUE_HEADS, HEAD_SIZE).transpose(0, 2, 1, 3)
    value_head_rows = attention_values.reshape(batch_count, whole_span, KEY_VALUE_HEADS, HEAD_SIZE).transpose(0, 2, 1, 3)
    window_reaches = jnp.broadcast_to(key_window_length[None, :], (batch_count, KEY_VALUE_HEADS))
    outputs, maxima, sums = jax.vmap(jax.vmap(attend_forward))(query_block, key_head_rows, value_head_rows, window_reaches)
    out_float = outputs.reshape(batch_count, TEST_LANES, whole_span, HEAD_SIZE).astype(jnp.float32)
    mean_square = lax.optimization_barrier(jnp.sum(out_float * out_float, axis=(1, 3))) / width_all
    inverse = 1.0 / jnp.sqrt(mean_square + epsilon)
    normed = out_float * inverse[:, None, :, None]
    gain_rows = norm_gain.reshape(TEST_LANES, HEAD_SIZE)[None, :, None, :]
    ceiling = spike_levels.astype(jnp.float32).reshape(TEST_LANES, HEAD_SIZE)[None, :, None, :]
    bounded = jnp.tanh(normed * gain_rows / ceiling)
    spikes = (ceiling * bounded).astype(jnp.bfloat16)
    membrane_queries = lin_queries.reshape(batch_count, whole_span, TEST_LANES, HEAD_SIZE).transpose(0, 2, 1, 3)
    membrane_keys = lin_keys.reshape(batch_count, whole_span, TEST_LANES, HEAD_SIZE).transpose(0, 2, 1, 3)
    membrane = jax.vmap(jax.vmap(membrane_forward))(membrane_queries, membrane_keys, spikes, decay_logs)
    scale_out = 1.0 / jnp.sqrt(lax.optimization_barrier(jnp.mean(membrane * membrane, axis=-1)) + epsilon)
    unit_out = membrane * scale_out[..., None]
    layer_output = unit_out.astype(jnp.bfloat16).transpose(0, 2, 1, 3).reshape(batch_count, whole_span, width_all)
    incoming = cotangent.reshape(batch_count, whole_span, TEST_LANES, HEAD_SIZE).transpose(0, 2, 1, 3).astype(jnp.float32)
    membrane_grad = scale_out[..., None] * (incoming - unit_out * lax.optimization_barrier(jnp.mean(incoming * unit_out, axis=-1, keepdims=True)))
    spike_grad = jax.vmap(jax.vmap(membrane_backward))(membrane_queries, membrane_keys, decay_logs, membrane_grad)
    level_grad = spike_grad * (1.0 - bounded * bounded)
    gain_grads = lax.optimization_barrier(jnp.sum(level_grad * normed, axis=(0, 2))).reshape(width_all)
    normed_grad = level_grad * gain_rows
    slope_sum = lax.optimization_barrier(jnp.sum(normed_grad * normed, axis=(1, 3))) / width_all
    output_gradient = (inverse[:, None, :, None] * (normed_grad - normed * slope_sum[:, None, :, None])).astype(jnp.bfloat16)
    group_gradient = output_gradient.reshape(batch_count, KEY_VALUE_HEADS, head_groups, whole_span, HEAD_SIZE)
    query_parts, key_accumulator, value_accumulator = jax.vmap(jax.vmap(attend_backward))(query_block, key_head_rows, value_head_rows, group_gradient, maxima, sums, window_reaches)
    query_grads = query_parts.astype(jnp.bfloat16).transpose(0, 3, 1, 2, 4).reshape(batch_count, whole_span, width_all)
    key_gradient = key_accumulator.astype(jnp.bfloat16).transpose(0, 2, 1, 3).reshape(batch_count, whole_span, KEY_VALUE_HEADS * HEAD_SIZE)
    value_gradient = value_accumulator.astype(jnp.bfloat16).transpose(0, 2, 1, 3).reshape(batch_count, whole_span, KEY_VALUE_HEADS * HEAD_SIZE)
    return (layer_output, query_grads, key_gradient, value_gradient, gain_grads)
```

```python
import math

import jax
import jax.numpy as jnp
from jax import lax
from jax.sharding import PartitionSpec as P

HEAD_SIZE = 128
D = 3584
LONGEST_WINDOW = 512


precise = lax.Precision.HIGHEST
epsilon = 1e-06


def passed_along(block, axis, distance):
    devices = range(lax.axis_size(axis))
    route = [(i - distance, i) for i in devices if i - distance in devices]
    return lax.ppermute(block, axis, route)


def entering(value, axis, join, neutral, backward):
    count, mine = (lax.axis_size(axis), lax.axis_index(axis))
    if backward:
        mine = count - 1 - mine
    before = jax.tree.map(
        lambda part, zero: jnp.full_like(part, 0) + jnp.asarray(zero, part.dtype), value, neutral
    )
    covered = value
    distance = 1
    while distance < count:
        moved = passed_along(covered, axis, -distance if backward else distance)
        present = mine >= distance
        before = jax.tree.map(
            lambda new, old: jnp.where(present, new, old), join(moved, before), before
        )
        if 2 * distance < count:
            covered = jax.tree.map(
                lambda new, old: jnp.where(present, new, old), join(moved, covered), covered
            )
        distance *= 2
    return before


def summed(value, axes):
    for axis in axes:
        count = lax.axis_size(axis)
        if count & (count - 1):
            value = lax.psum(value, axis)
            continue
        distance = 1
        while distance < count:
            value = value + lax.ppermute(
                value, axis, [(i, i ^ distance) for i in range(count)]
            )
            distance *= 2
    return value


def head_logits(query_rows, key_row_block, first_query, key_reach, scaling):
    block_rows = query_rows.shape[0]
    key_span = key_row_block.shape[0] - block_rows
    logits = (
        jnp.einsum("sd,kd->sk", query_rows, key_row_block, preferred_element_type=jnp.float32)
        * scaling
    )
    query_pos = first_query + jnp.arange(block_rows, dtype=jnp.int32)[:, None]
    key_pos = first_query - key_span + jnp.arange(key_row_block.shape[0], dtype=jnp.int32)[None, :]
    allowed = (key_pos >= 0) & (key_pos <= query_pos) & (key_pos > query_pos - key_reach)
    return jnp.where(allowed, logits, -jnp.inf)


def chain_states(earlier, later):
    return (earlier[0] * later[0], later[0][:, None, None] * earlier[1] + later[1])


def local(
    attention_queries,
    attention_keys,
    attention_values,
    key_window_length,
    norm_gain,
    spike_levels,
    lin_queries,
    lin_keys,
    decay_logs,
    cotangent,
):
    block_rows = attention_queries.shape[1]
    q_heads = attention_queries.shape[2] // HEAD_SIZE
    kv_heads = attention_keys.shape[2] // HEAD_SIZE
    head_groups = q_heads // kv_heads
    previous = (LONGEST_WINDOW + block_rows - 1) // block_rows
    key_span = previous * block_rows
    first_query = lax.axis_index("seq") * block_rows
    scaling = 1.0 / math.sqrt(HEAD_SIZE)
    own_pair = jnp.stack([attention_keys, attention_values])
    earlier_blocks = [passed_along(own_pair, "seq", distance) for distance in range(previous, 0, -1)]
    window_pair = jnp.concatenate(earlier_blocks + [own_pair], axis=2)
    window_pair = window_pair.reshape(2, key_span + block_rows, kv_heads, HEAD_SIZE).transpose(
        0, 2, 1, 3
    )
    window_keys = window_pair[0]
    window_values = window_pair[1]
    head_queries = attention_queries[0].reshape(block_rows, q_heads, HEAD_SIZE).transpose(1, 0, 2)
    kv_of_head = jnp.arange(q_heads, dtype=jnp.int32) // head_groups

    def forward_head(operands):
        query_rows, kv_index = operands
        key_row_block = lax.dynamic_index_in_dim(window_keys, kv_index, 0, keepdims=False)
        value_rows = lax.dynamic_index_in_dim(window_values, kv_index, 0, keepdims=False)
        key_reach = lax.dynamic_index_in_dim(key_window_length, kv_index, 0, keepdims=False)
        logits = head_logits(query_rows, key_row_block, first_query, key_reach, scaling)
        row_max = jnp.max(logits, axis=-1)
        exponent = jnp.exp(logits - row_max[:, None])
        row_sum = jnp.sum(exponent, axis=-1)
        weights = (exponent / row_sum[:, None]).astype(jnp.bfloat16)
        head_output = jnp.dot(weights, value_rows, preferred_element_type=jnp.float32).astype(
            jnp.bfloat16
        )
        return (head_output, row_max, row_sum)

    heads_out, maxima, sums = lax.map(forward_head, (head_queries, kv_of_head))
    out_float = heads_out.astype(jnp.float32)
    square_sum = summed(jnp.sum(out_float * out_float, axis=(0, 2)), ("tensor",))
    inverse = 1.0 / jnp.sqrt(square_sum / D + epsilon)
    normed = out_float * inverse[None, :, None]
    gain_rows = norm_gain.reshape(q_heads, HEAD_SIZE)[:, None, :]
    ceiling = spike_levels.astype(jnp.float32).reshape(q_heads, HEAD_SIZE)[:, None, :]
    bounded = jnp.tanh(normed * gain_rows / ceiling)
    spikes = (ceiling * bounded).astype(jnp.bfloat16)
    membrane_queries = lin_queries[0].reshape(block_rows, q_heads, HEAD_SIZE).transpose(1, 0, 2)
    membrane_keys = lin_keys[0].reshape(block_rows, q_heads, HEAD_SIZE).transpose(1, 0, 2)
    cumulative = jnp.cumsum(decay_logs[0], axis=1)
    lower_mask = jnp.arange(block_rows)[:, None] >= jnp.arange(block_rows)[None, :]
    gaps = jnp.where(lower_mask[None], cumulative[:, :, None] - cumulative[:, None, :], 0.0)
    products = jnp.einsum(
        "hsd,htd->hst", membrane_queries, membrane_keys, preferred_element_type=jnp.float32
    )
    decayed = jnp.where(lower_mask[None], jnp.exp(gaps), 0.0) * products
    spike_float = spikes.astype(jnp.float32)
    query_float = membrane_queries.astype(jnp.float32)
    key_float = membrane_keys.astype(jnp.float32)
    block_decay = jnp.exp(cumulative[:, -1])
    tail_decay = jnp.exp(cumulative[:, -1:] - cumulative)
    local_state = jnp.einsum(
        "hsd,hse->hde", key_float * tail_decay[..., None], spike_float, precision=precise
    )
    identity = (jnp.ones_like(block_decay), jnp.zeros_like(local_state))
    decay_before, state_in = entering(
        (block_decay, local_state), "seq", chain_states, identity, False
    )
    carried = jnp.einsum("hsd,hde->hse", query_float, state_in, precision=precise)
    membrane = (
        jnp.einsum("hst,htd->hsd", decayed, spike_float, precision=precise)
        + jnp.exp(cumulative)[..., None] * carried
    )
    scale_out = 1.0 / jnp.sqrt(jnp.mean(membrane * membrane, axis=-1) + epsilon)
    unit_out = membrane * scale_out[..., None]
    layer_output = (
        unit_out.astype(jnp.bfloat16).transpose(1, 0, 2).reshape(1, block_rows, q_heads * HEAD_SIZE)
    )
    incoming = (
        cotangent[0].reshape(block_rows, q_heads, HEAD_SIZE).transpose(1, 0, 2).astype(jnp.float32)
    )
    membrane_grad = scale_out[..., None] * (
        incoming - unit_out * jnp.mean(incoming * unit_out, axis=-1, keepdims=True)
    )
    head_part = jnp.einsum(
        "hsd,hse->hde",
        query_float * jnp.exp(cumulative)[..., None],
        membrane_grad,
        precision=precise,
    )
    decay_after, state_after = entering(
        (block_decay, head_part), "seq", chain_states, identity, True
    )
    later_part = jnp.einsum("htd,hde->hte", key_float, state_after, precision=precise)
    spike_grad = (
        jnp.einsum("hst,hsd->htd", decayed, membrane_grad, precision=precise)
        + tail_decay[..., None] * later_part
    )
    level_grad = spike_grad * (1.0 - bounded * bounded)
    gain_part = jnp.sum(level_grad * normed, axis=1).reshape(q_heads * HEAD_SIZE)
    gain_grads = summed(gain_part, ("seq", "dp"))
    normed_grad = level_grad * gain_rows
    slope_sum = summed(jnp.sum(normed_grad * normed, axis=(0, 2)), ("tensor",))
    output_gradient = (
        inverse[None, :, None] * (normed_grad - normed * (slope_sum / D)[None, :, None])
    ).astype(jnp.bfloat16)

    def backward_head(operands):
        query_rows, grad_rows, row_max, row_sum, kv_index = operands
        key_row_block = lax.dynamic_index_in_dim(window_keys, kv_index, 0, keepdims=False)
        value_rows = lax.dynamic_index_in_dim(window_values, kv_index, 0, keepdims=False)
        key_reach = lax.dynamic_index_in_dim(key_window_length, kv_index, 0, keepdims=False)
        logits = head_logits(query_rows, key_row_block, first_query, key_reach, scaling)
        probs = jnp.exp(logits - row_max[:, None]) / row_sum[:, None]
        weights = probs.astype(jnp.bfloat16)
        prob_grad = jnp.einsum(
            "sd,kd->sk", grad_rows, value_rows, preferred_element_type=jnp.float32
        )
        row_delta = jnp.sum(probs * prob_grad, axis=-1, keepdims=True)
        logit_grad = (probs * (prob_grad - row_delta) * scaling).astype(jnp.bfloat16)
        query_grad = jnp.dot(logit_grad, key_row_block, preferred_element_type=jnp.float32)
        key_part = jnp.einsum(
            "sk,sd->kd", logit_grad, query_rows, preferred_element_type=jnp.float32
        )
        value_part = jnp.einsum("sk,sd->kd", weights, grad_rows, preferred_element_type=jnp.float32)
        return (query_grad, key_part, value_part)

    query_parts, key_parts, value_parts = lax.map(
        backward_head, (head_queries, output_gradient, maxima, sums, kv_of_head)
    )
    key_sum = key_parts.reshape(kv_heads, head_groups, key_span + block_rows, HEAD_SIZE).sum(axis=1)
    value_sum = value_parts.reshape(kv_heads, head_groups, key_span + block_rows, HEAD_SIZE).sum(
        axis=1
    )
    pair_grads = jnp.stack([key_sum, value_sum])
    own_grads = pair_grads[:, :, key_span:]
    total_grads = own_grads
    for distance in range(previous, 0, -1):
        offset = (previous - distance) * block_rows
        total_grads = total_grads + passed_along(
            pair_grads[:, :, offset : offset + block_rows], "seq", -distance
        )
    query_grads = (
        query_parts.astype(jnp.bfloat16)
        .transpose(1, 0, 2)
        .reshape(1, block_rows, q_heads * HEAD_SIZE)
    )
    key_gradient = (
        total_grads[0]
        .astype(jnp.bfloat16)
        .transpose(1, 0, 2)
        .reshape(1, block_rows, kv_heads * HEAD_SIZE)
    )
    value_gradient = (
        total_grads[1]
        .astype(jnp.bfloat16)
        .transpose(1, 0, 2)
        .reshape(1, block_rows, kv_heads * HEAD_SIZE)
    )
    return (layer_output, query_grads, key_gradient, value_gradient, gain_grads)


def solution(mesh):
    placed = (
        P("dp", "seq", "tensor"),
        P("dp", "seq", "tensor"),
        P("dp", "seq", "tensor"),
        P("tensor"),
        P("tensor"),
        P("tensor"),
        P("dp", "seq", "tensor"),
        P("dp", "seq", "tensor"),
        P("dp", "tensor", "seq"),
        P("dp", "seq", "tensor"),
    )
    return jax.shard_map(
        local,
        mesh=mesh,
        in_specs=placed,
        out_specs=(
            P("dp", "seq", "tensor"),
            P("dp", "seq", "tensor"),
            P("dp", "seq", "tensor"),
            P("dp", "seq", "tensor"),
            P("tensor"),
        ),
        check_vma=False,
    )
```

```python
import math

import jax
import jax.numpy as jnp
from jax import lax
from jax.sharding import PartitionSpec as P

HEAD_SIZE = 128
D = 3584
LONGEST_WINDOW = 512
HEAD_SPLITS = 2


precise = lax.Precision.HIGHEST
epsilon = 1e-06


def passed_along(block, axis, distance):
    devices = range(lax.axis_size(axis))
    route = [(i - distance, i) for i in devices if i - distance in devices]
    return lax.ppermute(block, axis, route)


def chain_states(earlier, later):
    return (earlier[0] * later[0], later[0][:, None, None] * earlier[1] + later[1])


def picked(flag, new, old):
    return jax.tree.map(lambda a, b: jnp.where(flag, a, b), new, old)


def moved_on(value, axis, pairs):
    return lax.ppermute(value, axis, pairs)


def entering(value, axis, backward):
    count, index = (lax.axis_size(axis), lax.axis_index(axis))
    place = count - 1 - index if backward else index
    spot = (lambda p: count - 1 - p) if backward else (lambda p: p)
    identity = (jnp.ones_like(value[0]), jnp.zeros_like(value[1]))
    if count % 2:
        before, covered, distance = identity, value, 1
        while distance < count:
            moved = moved_on(
                covered, axis, [(spot(p), spot(p + distance)) for p in range(count - distance)]
            )
            present = place >= distance
            before = picked(present, chain_states(moved, before), before)
            covered = picked(present, chain_states(moved, covered), covered)
            distance *= 2
        return before[1]
    lead = place % 2 == 1
    first = moved_on(value, axis, [(spot(p), spot(p + 1)) for p in range(0, count, 2)])
    covered = chain_states(first, value)
    before = identity
    distance = 2
    while distance < count:
        moved = moved_on(
            covered,
            axis,
            [(spot(p), spot(p + distance)) for p in range(1, count - distance, 2)],
        )
        present = place >= distance
        before = picked(present, chain_states(moved, before), before)
        if 2 * distance < count:
            covered = picked(present, chain_states(moved, covered), covered)
        distance *= 2
    handed = moved_on(before[1], axis, [(spot(p), spot(p - 1)) for p in range(1, count, 2)])
    own_lead = chain_states(before, first)[1]
    return jnp.where(lead, own_lead, handed)


def summed(value, axes):
    for axis in axes:
        count = lax.axis_size(axis)
        if count & (count - 1):
            value = lax.psum(value, axis)
            continue
        distance = 1
        while distance < count:
            value = value + lax.ppermute(value, axis, [(i, i ^ distance) for i in range(count)])
            distance *= 2
    return value


def local(
    attention_queries,
    attention_keys,
    attention_values,
    key_window_length,
    norm_gain,
    spike_levels,
    lin_queries,
    lin_keys,
    decay_logs,
    cotangent,
):
    block_rows = attention_queries.shape[1]
    q_heads = attention_queries.shape[2] // HEAD_SIZE
    kv_heads = attention_keys.shape[2] // HEAD_SIZE
    head_groups = q_heads // kv_heads
    previous = (LONGEST_WINDOW + block_rows - 1) // block_rows
    key_span = previous * block_rows
    window = key_span + block_rows
    first_query = lax.axis_index("seq") * block_rows
    scaling = 1.0 / math.sqrt(HEAD_SIZE)
    own_pair = jnp.stack([attention_keys, attention_values])
    earlier_blocks = [passed_along(own_pair, "seq", distance) for distance in range(previous, 0, -1)]
    window_pair = jnp.concatenate(earlier_blocks + [own_pair], axis=2)
    window_pair = window_pair.reshape(2, window, kv_heads, HEAD_SIZE).transpose(0, 2, 1, 3)
    window_keys = window_pair[0]
    window_values = window_pair[1]
    head_queries = attention_queries[0].reshape(block_rows, q_heads, HEAD_SIZE).transpose(1, 0, 2)
    group_queries = head_queries.reshape(kv_heads, head_groups, block_rows, HEAD_SIZE)

    query_pos = first_query + jnp.arange(block_rows, dtype=jnp.int32)[:, None]
    key_pos = first_query - key_span + jnp.arange(window, dtype=jnp.int32)[None, :]
    reach = key_window_length[:, None, None, None]
    allowed = (
        (key_pos >= 0)[None, None]
        & (key_pos <= query_pos)[None, None]
        & (key_pos[None, None] > query_pos[None, None] - reach)
    )
    logits = (
        jnp.einsum(
            "gjsd,gkd->gjsk", group_queries, window_keys, preferred_element_type=jnp.float32
        )
        * scaling
    )
    logits = jnp.where(allowed, logits, -jnp.inf)
    row_max = jnp.max(logits, axis=-1, keepdims=True)
    exponent = jnp.exp(logits - row_max)
    row_sum = jnp.sum(exponent, axis=-1, keepdims=True)
    probs = exponent / row_sum
    weights = probs.astype(jnp.bfloat16)
    heads_out = (
        jnp.einsum("gjsk,gkd->gjsd", weights, window_values, preferred_element_type=jnp.float32)
        .astype(jnp.bfloat16)
        .reshape(q_heads, block_rows, HEAD_SIZE)
    )

    out_float = heads_out.astype(jnp.float32)
    square_sum = summed(jnp.sum(out_float * out_float, axis=(0, 2)), ("tensor",))
    inverse = 1.0 / jnp.sqrt(square_sum / D + epsilon)
    normed = out_float * inverse[None, :, None]
    gain_rows = norm_gain.reshape(q_heads, HEAD_SIZE)[:, None, :]
    ceiling = spike_levels.astype(jnp.float32).reshape(q_heads, HEAD_SIZE)[:, None, :]
    bounded = jnp.tanh(normed * gain_rows / ceiling)
    spikes = (ceiling * bounded).astype(jnp.bfloat16)
    membrane_queries = lin_queries[0].reshape(block_rows, q_heads, HEAD_SIZE).transpose(1, 0, 2)
    membrane_keys = lin_keys[0].reshape(block_rows, q_heads, HEAD_SIZE).transpose(1, 0, 2)
    cumulative = jnp.cumsum(decay_logs[0], axis=1)
    lower_mask = jnp.arange(block_rows)[:, None] >= jnp.arange(block_rows)[None, :]
    gaps = jnp.where(lower_mask[None], cumulative[:, :, None] - cumulative[:, None, :], 0.0)
    products = jnp.einsum(
        "hsd,htd->hst", membrane_queries, membrane_keys, preferred_element_type=jnp.float32
    )
    decayed = jnp.where(lower_mask[None], jnp.exp(gaps), 0.0) * products
    spike_float = spikes.astype(jnp.float32)
    query_float = membrane_queries.astype(jnp.float32)
    key_float = membrane_keys.astype(jnp.float32)
    block_decay = jnp.exp(cumulative[:, -1])
    tail_decay = jnp.exp(cumulative[:, -1:] - cumulative)
    head_decay = jnp.exp(cumulative)
    local_state = jnp.einsum(
        "hsd,hse->hde", key_float * tail_decay[..., None], spike_float, precision=precise
    )
    incoming = (
        cotangent[0].reshape(block_rows, q_heads, HEAD_SIZE).transpose(1, 0, 2).astype(jnp.float32)
    )

    splits = min(HEAD_SPLITS, q_heads)
    bounds = [q_heads * part // splits for part in range(splits + 1)]
    unit_parts, grad_parts = [], []
    for low, high in zip(bounds[:-1], bounds[1:]):
        part = slice(low, high)
        state_in = entering((block_decay[part], local_state[part]), "seq", False)
        carried = jnp.einsum("hsd,hde->hse", query_float[part], state_in, precision=precise)
        membrane = (
            jnp.einsum("hst,htd->hsd", decayed[part], spike_float[part], precision=precise)
            + head_decay[part][..., None] * carried
        )
        scale_out = 1.0 / jnp.sqrt(jnp.mean(membrane * membrane, axis=-1) + epsilon)
        unit_out = membrane * scale_out[..., None]
        membrane_grad = scale_out[..., None] * (
            incoming[part] - unit_out * jnp.mean(incoming[part] * unit_out, axis=-1, keepdims=True)
        )
        head_part = jnp.einsum(
            "hsd,hse->hde",
            query_float[part] * head_decay[part][..., None],
            membrane_grad,
            precision=precise,
        )
        state_after = entering((block_decay[part], head_part), "seq", True)
        later_part = jnp.einsum("htd,hde->hte", key_float[part], state_after, precision=precise)
        spike_grad = (
            jnp.einsum("hst,hsd->htd", decayed[part], membrane_grad, precision=precise)
            + tail_decay[part][..., None] * later_part
        )
        unit_parts.append(unit_out)
        grad_parts.append(spike_grad)
    unit_out = jnp.concatenate(unit_parts, axis=0)
    spike_grad = jnp.concatenate(grad_parts, axis=0)
    layer_output = (
        unit_out.astype(jnp.bfloat16).transpose(1, 0, 2).reshape(1, block_rows, q_heads * HEAD_SIZE)
    )
    level_grad = spike_grad * (1.0 - bounded * bounded)
    gain_part = jnp.sum(level_grad * normed, axis=1).reshape(q_heads * HEAD_SIZE)
    gain_grads = summed(gain_part, ("seq", "dp"))
    normed_grad = level_grad * gain_rows
    slope_sum = summed(jnp.sum(normed_grad * normed, axis=(0, 2)), ("tensor",))
    output_gradient = (
        inverse[None, :, None] * (normed_grad - normed * (slope_sum / D)[None, :, None])
    ).astype(jnp.bfloat16)

    grad_rows = output_gradient.reshape(kv_heads, head_groups, block_rows, HEAD_SIZE)
    prob_grad = jnp.einsum(
        "gjsd,gkd->gjsk", grad_rows, window_values, preferred_element_type=jnp.float32
    )
    row_delta = jnp.sum(probs * prob_grad, axis=-1, keepdims=True)
    logit_grad = (probs * (prob_grad - row_delta) * scaling).astype(jnp.bfloat16)
    query_parts = jnp.einsum(
        "gjsk,gkd->gjsd", logit_grad, window_keys, preferred_element_type=jnp.float32
    ).reshape(q_heads, block_rows, HEAD_SIZE)
    key_sum = jnp.einsum(
        "gjsk,gjsd->gkd", logit_grad, group_queries, preferred_element_type=jnp.float32
    )
    value_sum = jnp.einsum(
        "gjsk,gjsd->gkd", weights, grad_rows, preferred_element_type=jnp.float32
    )
    pair_grads = jnp.stack([key_sum, value_sum])
    total_grads = pair_grads[:, :, key_span:]
    for distance in range(previous, 0, -1):
        offset = (previous - distance) * block_rows
        total_grads = total_grads + passed_along(
            pair_grads[:, :, offset : offset + block_rows], "seq", -distance
        )
    query_grads = (
        query_parts.astype(jnp.bfloat16)
        .transpose(1, 0, 2)
        .reshape(1, block_rows, q_heads * HEAD_SIZE)
    )
    key_gradient = (
        total_grads[0]
        .astype(jnp.bfloat16)
        .transpose(1, 0, 2)
        .reshape(1, block_rows, kv_heads * HEAD_SIZE)
    )
    value_gradient = (
        total_grads[1]
        .astype(jnp.bfloat16)
        .transpose(1, 0, 2)
        .reshape(1, block_rows, kv_heads * HEAD_SIZE)
    )
    return (layer_output, query_grads, key_gradient, value_gradient, gain_grads)


def solution(mesh):
    placed = (
        P("dp", "seq", "tensor"),
        P("dp", "seq", "tensor"),
        P("dp", "seq", "tensor"),
        P("tensor"),
        P("tensor"),
        P("tensor"),
        P("dp", "seq", "tensor"),
        P("dp", "seq", "tensor"),
        P("dp", "tensor", "seq"),
        P("dp", "seq", "tensor"),
    )
    return jax.shard_map(
        local,
        mesh=mesh,
        in_specs=placed,
        out_specs=(
            P("dp", "seq", "tensor"),
            P("dp", "seq", "tensor"),
            P("dp", "seq", "tensor"),
            P("dp", "seq", "tensor"),
            P("tensor"),
        ),
        check_vma=False,
    )
```

```python
import math

import jax
import jax.numpy as jnp
from jax import lax
from jax.sharding import PartitionSpec as P

HEAD_SIZE = 128
D = 3584
LONGEST_WINDOW = 512
HEAD_SPLITS = 2


precise = lax.Precision.HIGHEST
epsilon = 1e-06


def passed_along(block, axis, distance):
    devices = range(lax.axis_size(axis))
    route = [(i - distance, i) for i in devices if i - distance in devices]
    return lax.ppermute(block, axis, route)


def chain_states(earlier, later):
    rows = later.shape[1] - 8
    is_state = jnp.arange(later.shape[1])[None, :, None] < rows
    return jnp.where(is_state, later[:, rows : rows + 1, :1] * earlier + later, earlier * later)


def picked(flag, new, old):
    return jnp.where(flag, new, old)


def moved_on(value, axis, pairs):
    return lax.ppermute(value, axis, pairs)


def entering(decay, state, axis, backward):
    count, index = (lax.axis_size(axis), lax.axis_index(axis))
    place = count - 1 - index if backward else index
    spot = (lambda p: count - 1 - p) if backward else (lambda p: p)
    rows = state.shape[1]
    value = jnp.concatenate(
        [state, jnp.broadcast_to(decay[:, None, None], (state.shape[0], 8, state.shape[2]))], axis=1
    )
    identity = jnp.concatenate([jnp.zeros_like(state), jnp.ones_like(value[:, rows:])], axis=1)
    if count % 2:
        before, covered, distance = identity, value, 1
        while distance < count:
            moved = moved_on(
                covered, axis, [(spot(p), spot(p + distance)) for p in range(count - distance)]
            )
            present = place >= distance
            before = picked(present, chain_states(moved, before), before)
            covered = picked(present, chain_states(moved, covered), covered)
            distance *= 2
        return before[:, :rows]
    lead = place % 2 == 1
    first = moved_on(value, axis, [(spot(p), spot(p + 1)) for p in range(0, count, 2)])
    covered = chain_states(first, value)
    before = identity
    distance = 2
    while distance < count:
        moved = moved_on(
            covered,
            axis,
            [(spot(p), spot(p + distance)) for p in range(1, count - distance, 2)],
        )
        present = place >= distance
        before = picked(present, chain_states(moved, before), before)
        if 2 * distance < count:
            covered = picked(present, chain_states(moved, covered), covered)
        distance *= 2
    handed = moved_on(before[:, :rows], axis, [(spot(p), spot(p - 1)) for p in range(1, count, 2)])
    own_lead = chain_states(before, first)[:, :rows]
    return jnp.where(lead, own_lead, handed)


def summed(value, axes):
    for axis in axes:
        count = lax.axis_size(axis)
        if count & (count - 1):
            value = lax.psum(value, axis)
            continue
        distance = 1
        while distance < count:
            value = value + lax.ppermute(value, axis, [(i, i ^ distance) for i in range(count)])
            distance *= 2
    return value


def local(
    attention_queries,
    attention_keys,
    attention_values,
    key_window_length,
    norm_gain,
    spike_levels,
    lin_queries,
    lin_keys,
    decay_logs,
    cotangent,
):
    block_rows = attention_queries.shape[1]
    q_heads = attention_queries.shape[2] // HEAD_SIZE
    kv_heads = attention_keys.shape[2] // HEAD_SIZE
    head_groups = q_heads // kv_heads
    previous = (LONGEST_WINDOW + block_rows - 1) // block_rows
    key_span = previous * block_rows
    window = key_span + block_rows
    first_query = lax.axis_index("seq") * block_rows
    scaling = 1.0 / math.sqrt(HEAD_SIZE)
    own_pair = jnp.stack([attention_keys, attention_values])
    earlier_blocks = [passed_along(own_pair, "seq", distance) for distance in range(previous, 0, -1)]
    window_pair = jnp.concatenate(earlier_blocks + [own_pair], axis=2)
    window_pair = window_pair.reshape(2, window, kv_heads, HEAD_SIZE).transpose(0, 2, 1, 3)
    window_keys = window_pair[0]
    window_values = window_pair[1]
    head_queries = attention_queries[0].reshape(block_rows, q_heads, HEAD_SIZE).transpose(1, 0, 2)
    group_queries = head_queries.reshape(kv_heads, head_groups, block_rows, HEAD_SIZE)

    query_pos = first_query + jnp.arange(block_rows, dtype=jnp.int32)[:, None]
    key_pos = first_query - key_span + jnp.arange(window, dtype=jnp.int32)[None, :]
    reach = key_window_length[:, None, None, None]
    allowed = (
        (key_pos >= 0)[None, None]
        & (key_pos <= query_pos)[None, None]
        & (key_pos[None, None] > query_pos[None, None] - reach)
    )
    logits = (
        jnp.einsum(
            "gjsd,gkd->gjsk", group_queries, window_keys, preferred_element_type=jnp.float32
        )
        * scaling
    )
    logits = jnp.where(allowed, logits, -jnp.inf)
    row_max = jnp.max(logits, axis=-1, keepdims=True)
    exponent = jnp.exp(logits - row_max)
    row_sum = jnp.sum(exponent, axis=-1, keepdims=True)
    probs = exponent / row_sum
    weights = probs.astype(jnp.bfloat16)
    heads_out = (
        jnp.einsum("gjsk,gkd->gjsd", weights, window_values, preferred_element_type=jnp.float32)
        .astype(jnp.bfloat16)
        .reshape(q_heads, block_rows, HEAD_SIZE)
    )

    out_float = heads_out.astype(jnp.float32)
    square_sum = summed(jnp.sum(out_float * out_float, axis=(0, 2)), ("tensor",))
    inverse = 1.0 / jnp.sqrt(square_sum / D + epsilon)
    normed = out_float * inverse[None, :, None]
    gain_rows = norm_gain.reshape(q_heads, HEAD_SIZE)[:, None, :]
    ceiling = spike_levels.astype(jnp.float32).reshape(q_heads, HEAD_SIZE)[:, None, :]
    bounded = jnp.tanh(normed * gain_rows / ceiling)
    spikes = (ceiling * bounded).astype(jnp.bfloat16)
    membrane_queries = lin_queries[0].reshape(block_rows, q_heads, HEAD_SIZE).transpose(1, 0, 2)
    membrane_keys = lin_keys[0].reshape(block_rows, q_heads, HEAD_SIZE).transpose(1, 0, 2)
    cumulative = jnp.cumsum(decay_logs[0], axis=1)
    lower_mask = jnp.arange(block_rows)[:, None] >= jnp.arange(block_rows)[None, :]
    gaps = jnp.where(lower_mask[None], cumulative[:, :, None] - cumulative[:, None, :], 0.0)
    products = jnp.einsum(
        "hsd,htd->hst", membrane_queries, membrane_keys, preferred_element_type=jnp.float32
    )
    decayed = jnp.where(lower_mask[None], jnp.exp(gaps), 0.0) * products
    spike_float = spikes.astype(jnp.float32)
    query_float = membrane_queries.astype(jnp.float32)
    key_float = membrane_keys.astype(jnp.float32)
    block_decay = jnp.exp(cumulative[:, -1])
    tail_decay = jnp.exp(cumulative[:, -1:] - cumulative)
    head_decay = jnp.exp(cumulative)
    local_state = jnp.einsum(
        "hsd,hse->hde", key_float * tail_decay[..., None], spike_float, precision=precise
    )
    incoming = (
        cotangent[0].reshape(block_rows, q_heads, HEAD_SIZE).transpose(1, 0, 2).astype(jnp.float32)
    )

    splits = min(HEAD_SPLITS, q_heads)
    bounds = [q_heads * part // splits for part in range(splits + 1)]
    unit_parts, grad_parts, gain_parts = [], [], []
    state_in = None
    for low, high in zip(bounds[:-1], bounds[1:]):
        part = slice(low, high)
        part_state = local_state[part]
        if state_in is not None:
            part_state, _ = lax.optimization_barrier((part_state, state_in))
        state_in = entering(block_decay[part], part_state, "seq", False)
        carried = jnp.einsum("hsd,hde->hse", query_float[part], state_in, precision=precise)
        membrane = (
            jnp.einsum("hst,htd->hsd", decayed[part], spike_float[part], precision=precise)
            + head_decay[part][..., None] * carried
        )
        scale_out = 1.0 / jnp.sqrt(jnp.mean(membrane * membrane, axis=-1) + epsilon)
        unit_out = membrane * scale_out[..., None]
        membrane_grad = scale_out[..., None] * (
            incoming[part] - unit_out * jnp.mean(incoming[part] * unit_out, axis=-1, keepdims=True)
        )
        head_part = jnp.einsum(
            "hsd,hse->hde",
            query_float[part] * head_decay[part][..., None],
            membrane_grad,
            precision=precise,
        )
        state_after = entering(block_decay[part], head_part, "seq", True)
        later_part = jnp.einsum("htd,hde->hte", key_float[part], state_after, precision=precise)
        spike_grad = (
            jnp.einsum("hst,hsd->htd", decayed[part], membrane_grad, precision=precise)
            + tail_decay[part][..., None] * later_part
        )
        part_level = spike_grad * (1.0 - bounded[part] * bounded[part])
        part_gain = jnp.sum(part_level * normed[part], axis=1).reshape((high - low) * HEAD_SIZE)
        gain_parts.append(jnp.sum(lax.all_gather(part_gain, ("seq", "dp")), axis=0))
        unit_parts.append(unit_out)
        grad_parts.append(part_level)
    unit_out = jnp.concatenate(unit_parts, axis=0)
    level_grad = jnp.concatenate(grad_parts, axis=0)
    gain_grads = jnp.concatenate(gain_parts, axis=0)
    layer_output = (
        unit_out.astype(jnp.bfloat16).transpose(1, 0, 2).reshape(1, block_rows, q_heads * HEAD_SIZE)
    )
    normed_grad = level_grad * gain_rows
    slope_sum = summed(jnp.sum(normed_grad * normed, axis=(0, 2)), ("tensor",))
    output_gradient = (
        inverse[None, :, None] * (normed_grad - normed * (slope_sum / D)[None, :, None])
    ).astype(jnp.bfloat16)

    grad_rows = output_gradient.reshape(kv_heads, head_groups, block_rows, HEAD_SIZE)
    prob_grad = jnp.einsum(
        "gjsd,gkd->gjsk", grad_rows, window_values, preferred_element_type=jnp.float32
    )
    row_delta = jnp.sum(probs * prob_grad, axis=-1, keepdims=True)
    logit_grad = (probs * (prob_grad - row_delta) * scaling).astype(jnp.bfloat16)
    query_parts = jnp.einsum(
        "gjsk,gkd->gjsd", logit_grad, window_keys, preferred_element_type=jnp.float32
    ).reshape(q_heads, block_rows, HEAD_SIZE)
    key_sum = jnp.einsum(
        "gjsk,gjsd->gkd", logit_grad, group_queries, preferred_element_type=jnp.float32
    )
    value_sum = jnp.einsum(
        "gjsk,gjsd->gkd", weights, grad_rows, preferred_element_type=jnp.float32
    )
    pair_grads = jnp.stack([key_sum, value_sum])
    total_grads = pair_grads[:, :, key_span:]
    for distance in range(previous, 0, -1):
        offset = (previous - distance) * block_rows
        total_grads = total_grads + passed_along(
            pair_grads[:, :, offset : offset + block_rows], "seq", -distance
        )
    query_grads = (
        query_parts.astype(jnp.bfloat16)
        .transpose(1, 0, 2)
        .reshape(1, block_rows, q_heads * HEAD_SIZE)
    )
    key_gradient = (
        total_grads[0]
        .astype(jnp.bfloat16)
        .transpose(1, 0, 2)
        .reshape(1, block_rows, kv_heads * HEAD_SIZE)
    )
    value_gradient = (
        total_grads[1]
        .astype(jnp.bfloat16)
        .transpose(1, 0, 2)
        .reshape(1, block_rows, kv_heads * HEAD_SIZE)
    )
    return (layer_output, query_grads, key_gradient, value_gradient, gain_grads)


def solution(mesh):
    placed = (
        P("dp", "seq", "tensor"),
        P("dp", "seq", "tensor"),
        P("dp", "seq", "tensor"),
        P("tensor"),
        P("tensor"),
        P("tensor"),
        P("dp", "seq", "tensor"),
        P("dp", "seq", "tensor"),
        P("dp", "tensor", "seq"),
        P("dp", "seq", "tensor"),
    )
    return jax.shard_map(
        local,
        mesh=mesh,
        in_specs=placed,
        out_specs=(
            P("dp", "seq", "tensor"),
            P("dp", "seq", "tensor"),
            P("dp", "seq", "tensor"),
            P("dp", "seq", "tensor"),
            P("tensor"),
        ),
        check_vma=False,
    )
```

```python
import math

import jax
import jax.numpy as jnp
from jax import lax
from jax.sharding import PartitionSpec as P

HEAD_SIZE = 128
D = 3584
LONGEST_WINDOW = 512
HEAD_SPLITS = 2


precise = lax.Precision.HIGHEST
epsilon = 1e-06


def passed_along(block, axis, distance):
    devices = range(lax.axis_size(axis))
    route = [(i - distance, i) for i in devices if i - distance in devices]
    return lax.ppermute(block, axis, route)


def chain_states(earlier, later):
    rows = later.shape[1] - 8
    is_state = jnp.arange(later.shape[1])[None, :, None] < rows
    return jnp.where(is_state, later[:, rows : rows + 1, :1] * earlier + later, earlier * later)


def picked(flag, new, old):
    return jnp.where(flag, new, old)


def moved_on(value, axis, pairs):
    return lax.ppermute(value, axis, pairs)


def entering(decay, state, axis, backward):
    count, index = (lax.axis_size(axis), lax.axis_index(axis))
    place = count - 1 - index if backward else index
    spot = (lambda p: count - 1 - p) if backward else (lambda p: p)
    rows = state.shape[1]
    value = jnp.concatenate(
        [state, jnp.broadcast_to(decay[:, None, None], (state.shape[0], 8, state.shape[2]))], axis=1
    )
    identity = jnp.concatenate([jnp.zeros_like(state), jnp.ones_like(value[:, rows:])], axis=1)
    if count % 2:
        before, covered, distance = identity, value, 1
        while distance < count:
            moved = moved_on(
                covered, axis, [(spot(p), spot(p + distance)) for p in range(count - distance)]
            )
            present = place >= distance
            before = picked(present, chain_states(moved, before), before)
            covered = picked(present, chain_states(moved, covered), covered)
            distance *= 2
        return before[:, :rows]
    lead = place % 2 == 1
    first = moved_on(value, axis, [(spot(p), spot(p + 1)) for p in range(0, count, 2)])
    covered = chain_states(first, value)
    before = identity
    distance = 2
    while distance < count:
        sent = covered.astype(jnp.bfloat16) if distance >= 4 else covered
        moved = moved_on(
            sent,
            axis,
            [(spot(p), spot(p + distance)) for p in range(1, count - distance, 2)],
        ).astype(jnp.float32)
        present = place >= distance
        before = picked(present, chain_states(moved, before), before)
        if 2 * distance < count:
            covered = picked(present, chain_states(moved, covered), covered)
        distance *= 2
    handed = moved_on(before[:, :rows], axis, [(spot(p), spot(p - 1)) for p in range(1, count, 2)])
    own_lead = chain_states(before, first)[:, :rows]
    return jnp.where(lead, own_lead, handed)


def summed(value, axes):
    for axis in axes:
        count = lax.axis_size(axis)
        if count & (count - 1):
            value = lax.psum(value, axis)
            continue
        distance = 1
        while distance < count:
            value = value + lax.ppermute(value, axis, [(i, i ^ distance) for i in range(count)])
            distance *= 2
    return value


def local(
    attention_queries,
    attention_keys,
    attention_values,
    key_window_length,
    norm_gain,
    spike_levels,
    lin_queries,
    lin_keys,
    decay_logs,
    cotangent,
):
    block_rows = attention_queries.shape[1]
    q_heads = attention_queries.shape[2] // HEAD_SIZE
    kv_heads = attention_keys.shape[2] // HEAD_SIZE
    head_groups = q_heads // kv_heads
    previous = (LONGEST_WINDOW + block_rows - 1) // block_rows
    key_span = previous * block_rows
    window = key_span + block_rows
    first_query = lax.axis_index("seq") * block_rows
    scaling = 1.0 / math.sqrt(HEAD_SIZE)
    own_pair = jnp.stack([attention_keys, attention_values])
    earlier_blocks = [passed_along(own_pair, "seq", distance) for distance in range(previous, 0, -1)]
    window_pair = jnp.concatenate(earlier_blocks + [own_pair], axis=2)
    window_pair = window_pair.reshape(2, window, kv_heads, HEAD_SIZE).transpose(0, 2, 1, 3)
    window_keys = window_pair[0]
    window_values = window_pair[1]
    head_queries = attention_queries[0].reshape(block_rows, q_heads, HEAD_SIZE).transpose(1, 0, 2)
    group_queries = head_queries.reshape(kv_heads, head_groups, block_rows, HEAD_SIZE)

    query_pos = first_query + jnp.arange(block_rows, dtype=jnp.int32)[:, None]
    key_pos = first_query - key_span + jnp.arange(window, dtype=jnp.int32)[None, :]
    reach = key_window_length[:, None, None, None]
    allowed = (
        (key_pos >= 0)[None, None]
        & (key_pos <= query_pos)[None, None]
        & (key_pos[None, None] > query_pos[None, None] - reach)
    )
    logits = (
        jnp.einsum(
            "gjsd,gkd->gjsk", group_queries, window_keys, preferred_element_type=jnp.float32
        )
        * scaling
    )
    logits = jnp.where(allowed, logits, -jnp.inf)
    row_max = jnp.max(logits, axis=-1, keepdims=True)
    exponent = jnp.exp(logits - row_max)
    row_sum = jnp.sum(exponent, axis=-1, keepdims=True)
    probs = exponent / row_sum
    weights = probs.astype(jnp.bfloat16)
    heads_out = (
        jnp.einsum("gjsk,gkd->gjsd", weights, window_values, preferred_element_type=jnp.float32)
        .astype(jnp.bfloat16)
        .reshape(q_heads, block_rows, HEAD_SIZE)
    )

    out_float = heads_out.astype(jnp.float32)
    square_sum = summed(jnp.sum(out_float * out_float, axis=(0, 2)), ("tensor",))
    inverse = 1.0 / jnp.sqrt(square_sum / D + epsilon)
    normed = out_float * inverse[None, :, None]
    gain_rows = norm_gain.reshape(q_heads, HEAD_SIZE)[:, None, :]
    ceiling = spike_levels.astype(jnp.float32).reshape(q_heads, HEAD_SIZE)[:, None, :]
    bounded = jnp.tanh(normed * gain_rows / ceiling)
    spikes = (ceiling * bounded).astype(jnp.bfloat16)
    membrane_queries = lin_queries[0].reshape(block_rows, q_heads, HEAD_SIZE).transpose(1, 0, 2)
    membrane_keys = lin_keys[0].reshape(block_rows, q_heads, HEAD_SIZE).transpose(1, 0, 2)
    cumulative = jnp.cumsum(decay_logs[0], axis=1)
    lower_mask = jnp.arange(block_rows)[:, None] >= jnp.arange(block_rows)[None, :]
    gaps = jnp.where(lower_mask[None], cumulative[:, :, None] - cumulative[:, None, :], 0.0)
    products = jnp.einsum(
        "hsd,htd->hst", membrane_queries, membrane_keys, preferred_element_type=jnp.float32
    )
    decayed = jnp.where(lower_mask[None], jnp.exp(gaps), 0.0) * products
    spike_float = spikes.astype(jnp.float32)
    query_float = membrane_queries.astype(jnp.float32)
    key_float = membrane_keys.astype(jnp.float32)
    block_decay = jnp.exp(cumulative[:, -1])
    tail_decay = jnp.exp(cumulative[:, -1:] - cumulative)
    head_decay = jnp.exp(cumulative)
    local_state = jnp.einsum(
        "hsd,hse->hde", key_float * tail_decay[..., None], spike_float, precision=precise
    )
    incoming = (
        cotangent[0].reshape(block_rows, q_heads, HEAD_SIZE).transpose(1, 0, 2).astype(jnp.float32)
    )

    splits = min(HEAD_SPLITS, q_heads)
    bounds = [q_heads * part // splits for part in range(splits + 1)]
    unit_parts, grad_parts, gain_parts = [], [], []
    for low, high in zip(bounds[:-1], bounds[1:]):
        part = slice(low, high)
        state_in = entering(block_decay[part], local_state[part], "seq", False)
        carried = jnp.einsum("hsd,hde->hse", query_float[part], state_in, precision=precise)
        membrane = (
            jnp.einsum("hst,htd->hsd", decayed[part], spike_float[part], precision=precise)
            + head_decay[part][..., None] * carried
        )
        scale_out = 1.0 / jnp.sqrt(jnp.mean(membrane * membrane, axis=-1) + epsilon)
        unit_out = membrane * scale_out[..., None]
        membrane_grad = scale_out[..., None] * (
            incoming[part] - unit_out * jnp.mean(incoming[part] * unit_out, axis=-1, keepdims=True)
        )
        head_part = jnp.einsum(
            "hsd,hse->hde",
            query_float[part] * head_decay[part][..., None],
            membrane_grad,
            precision=precise,
        )
        state_after = entering(block_decay[part], head_part, "seq", True)
        later_part = jnp.einsum("htd,hde->hte", key_float[part], state_after, precision=precise)
        spike_grad = (
            jnp.einsum("hst,hsd->htd", decayed[part], membrane_grad, precision=precise)
            + tail_decay[part][..., None] * later_part
        )
        part_level = spike_grad * (1.0 - bounded[part] * bounded[part])
        part_gain = jnp.sum(part_level * normed[part], axis=1).reshape((high - low) * HEAD_SIZE)
        gain_parts.append(part_gain)
        unit_parts.append(unit_out)
        grad_parts.append(part_level)
    unit_out = jnp.concatenate(unit_parts, axis=0)
    level_grad = jnp.concatenate(grad_parts, axis=0)
    gain_grads = summed(jnp.concatenate(gain_parts, axis=0), ("seq", "dp"))
    layer_output = (
        unit_out.astype(jnp.bfloat16).transpose(1, 0, 2).reshape(1, block_rows, q_heads * HEAD_SIZE)
    )
    normed_grad = level_grad * gain_rows
    slope_sum = summed(jnp.sum(normed_grad * normed, axis=(0, 2)), ("tensor",))
    output_gradient = (
        inverse[None, :, None] * (normed_grad - normed * (slope_sum / D)[None, :, None])
    ).astype(jnp.bfloat16)

    grad_rows = output_gradient.reshape(kv_heads, head_groups, block_rows, HEAD_SIZE)
    prob_grad = jnp.einsum(
        "gjsd,gkd->gjsk", grad_rows, window_values, preferred_element_type=jnp.float32
    )
    row_delta = jnp.sum(probs * prob_grad, axis=-1, keepdims=True)
    logit_grad = (probs * (prob_grad - row_delta) * scaling).astype(jnp.bfloat16)
    query_parts = jnp.einsum(
        "gjsk,gkd->gjsd", logit_grad, window_keys, preferred_element_type=jnp.float32
    ).reshape(q_heads, block_rows, HEAD_SIZE)
    key_sum = jnp.einsum(
        "gjsk,gjsd->gkd", logit_grad, group_queries, preferred_element_type=jnp.float32
    )
    value_sum = jnp.einsum(
        "gjsk,gjsd->gkd", weights, grad_rows, preferred_element_type=jnp.float32
    )
    pair_grads = jnp.stack([key_sum, value_sum])
    total_grads = pair_grads[:, :, key_span:]
    for distance in range(previous, 0, -1):
        offset = (previous - distance) * block_rows
        total_grads = total_grads + passed_along(
            pair_grads[:, :, offset : offset + block_rows], "seq", -distance
        )
    query_grads = (
        query_parts.astype(jnp.bfloat16)
        .transpose(1, 0, 2)
        .reshape(1, block_rows, q_heads * HEAD_SIZE)
    )
    key_gradient = (
        total_grads[0]
        .astype(jnp.bfloat16)
        .transpose(1, 0, 2)
        .reshape(1, block_rows, kv_heads * HEAD_SIZE)
    )
    value_gradient = (
        total_grads[1]
        .astype(jnp.bfloat16)
        .transpose(1, 0, 2)
        .reshape(1, block_rows, kv_heads * HEAD_SIZE)
    )
    return (layer_output, query_grads, key_gradient, value_gradient, gain_grads)


def solution(mesh):
    placed = (
        P("dp", "seq", "tensor"),
        P("dp", "seq", "tensor"),
        P("dp", "seq", "tensor"),
        P("tensor"),
        P("tensor"),
        P("tensor"),
        P("dp", "seq", "tensor"),
        P("dp", "seq", "tensor"),
        P("dp", "tensor", "seq"),
        P("dp", "seq", "tensor"),
    )
    return jax.shard_map(
        local,
        mesh=mesh,
        in_specs=placed,
        out_specs=(
            P("dp", "seq", "tensor"),
            P("dp", "seq", "tensor"),
            P("dp", "seq", "tensor"),
            P("dp", "seq", "tensor"),
            P("tensor"),
        ),
        check_vma=False,
    )
```

```python
import math

import jax
import jax.numpy as jnp
from jax import lax
from jax.sharding import PartitionSpec as P

HEAD_SIZE = 128
D = 3584
LONGEST_WINDOW = 512
HEAD_SPLITS = 1


precise = lax.Precision.HIGHEST
epsilon = 1e-06


def passed_along(block, axis, distance):
    devices = range(lax.axis_size(axis))
    route = [(i - distance, i) for i in devices if i - distance in devices]
    return lax.ppermute(block, axis, route)


def chain_states(earlier, later):
    rows = later.shape[1] - 8
    is_state = jnp.arange(later.shape[1])[None, :, None] < rows
    return jnp.where(is_state, later[:, rows : rows + 1, :1] * earlier + later, earlier * later)


def picked(flag, new, old):
    return jnp.where(flag, new, old)


def moved_on(value, axis, pairs):
    return lax.ppermute(value, axis, pairs)


def entering(decay, state, axis, backward):
    count, index = (lax.axis_size(axis), lax.axis_index(axis))
    place = count - 1 - index if backward else index
    spot = (lambda p: count - 1 - p) if backward else (lambda p: p)
    rows = state.shape[1]
    value = jnp.concatenate(
        [state, jnp.broadcast_to(decay[:, None, None], (state.shape[0], 8, state.shape[2]))], axis=1
    )
    identity = jnp.concatenate([jnp.zeros_like(state), jnp.ones_like(value[:, rows:])], axis=1)
    if count % 2:
        before, covered, distance = identity, value, 1
        while distance < count:
            moved = moved_on(
                covered, axis, [(spot(p), spot(p + distance)) for p in range(count - distance)]
            )
            present = place >= distance
            before = picked(present, chain_states(moved, before), before)
            covered = picked(present, chain_states(moved, covered), covered)
            distance *= 2
        return before[:, :rows]
    lead = place % 2 == 1
    first = moved_on(value, axis, [(spot(p), spot(p + 1)) for p in range(0, count, 2)])
    covered = chain_states(first, value)
    before = identity
    distance = 2
    while distance < count:
        sent = covered.astype(jnp.bfloat16) if distance >= 4 else covered
        moved = moved_on(
            sent,
            axis,
            [(spot(p), spot(p + distance)) for p in range(1, count - distance, 2)],
        ).astype(jnp.float32)
        present = place >= distance
        before = picked(present, chain_states(moved, before), before)
        if 2 * distance < count:
            covered = picked(present, chain_states(moved, covered), covered)
        distance *= 2
    handed = moved_on(before[:, :rows], axis, [(spot(p), spot(p - 1)) for p in range(1, count, 2)])
    own_lead = chain_states(before, first)[:, :rows]
    return jnp.where(lead, own_lead, handed)


def xor_reduced(value, axis, offsets):
    count = lax.axis_size(axis)
    combos = [0]
    for offset in offsets:
        combos = combos + [c ^ offset for c in combos]
    values = {0: value}
    for c in combos[1:]:
        values[c] = lax.ppermute(value, axis, [(i, i ^ c) for i in range(count)])
    for offset in offsets:
        values = {c: values[c] + values[c ^ offset] for c in values if not c & offset}
    return values[0]


def summed(value, axes):
    for axis in axes:
        count = lax.axis_size(axis)
        if count & (count - 1):
            value = lax.psum(value, axis)
            continue
        bits = [1 << k for k in range(count.bit_length() - 1)]
        for low in range(0, len(bits), 3):
            value = xor_reduced(value, axis, bits[low : low + 3])
    return value


def local(
    attention_queries,
    attention_keys,
    attention_values,
    key_window_length,
    norm_gain,
    spike_levels,
    lin_queries,
    lin_keys,
    decay_logs,
    cotangent,
):
    block_rows = attention_queries.shape[1]
    q_heads = attention_queries.shape[2] // HEAD_SIZE
    kv_heads = attention_keys.shape[2] // HEAD_SIZE
    head_groups = q_heads // kv_heads
    previous = (LONGEST_WINDOW + block_rows - 1) // block_rows
    key_span = previous * block_rows
    window = key_span + block_rows
    first_query = lax.axis_index("seq") * block_rows
    scaling = 1.0 / math.sqrt(HEAD_SIZE)
    own_pair = jnp.stack([attention_keys, attention_values])
    earlier_blocks = [passed_along(own_pair, "seq", distance) for distance in range(previous, 0, -1)]
    window_pair = jnp.concatenate(earlier_blocks + [own_pair], axis=2)
    window_pair = window_pair.reshape(2, window, kv_heads, HEAD_SIZE).transpose(0, 2, 1, 3)
    window_keys = window_pair[0]
    window_values = window_pair[1]
    head_queries = attention_queries[0].reshape(block_rows, q_heads, HEAD_SIZE).transpose(1, 0, 2)
    group_queries = head_queries.reshape(kv_heads, head_groups, block_rows, HEAD_SIZE)

    query_pos = first_query + jnp.arange(block_rows, dtype=jnp.int32)[:, None]
    key_pos = first_query - key_span + jnp.arange(window, dtype=jnp.int32)[None, :]
    reach = key_window_length[:, None, None, None]
    allowed = (
        (key_pos >= 0)[None, None]
        & (key_pos <= query_pos)[None, None]
        & (key_pos[None, None] > query_pos[None, None] - reach)
    )
    logits = (
        jnp.einsum(
            "gjsd,gkd->gjsk", group_queries, window_keys, preferred_element_type=jnp.float32
        )
        * scaling
    )
    logits = jnp.where(allowed, logits, -jnp.inf)
    row_max = jnp.max(logits, axis=-1, keepdims=True)
    exponent = jnp.exp(logits - row_max)
    row_sum = jnp.sum(exponent, axis=-1, keepdims=True)
    probs = exponent / row_sum
    weights = probs.astype(jnp.bfloat16)
    heads_out = (
        jnp.einsum("gjsk,gkd->gjsd", weights, window_values, preferred_element_type=jnp.float32)
        .astype(jnp.bfloat16)
        .reshape(q_heads, block_rows, HEAD_SIZE)
    )

    out_float = heads_out.astype(jnp.float32)
    square_sum = summed(jnp.sum(out_float * out_float, axis=(0, 2)), ("tensor",))
    inverse = 1.0 / jnp.sqrt(square_sum / D + epsilon)
    normed = out_float * inverse[None, :, None]
    gain_rows = norm_gain.reshape(q_heads, HEAD_SIZE)[:, None, :]
    ceiling = spike_levels.astype(jnp.float32).reshape(q_heads, HEAD_SIZE)[:, None, :]
    bounded = jnp.tanh(normed * gain_rows / ceiling)
    spikes = (ceiling * bounded).astype(jnp.bfloat16)
    membrane_queries = lin_queries[0].reshape(block_rows, q_heads, HEAD_SIZE).transpose(1, 0, 2)
    membrane_keys = lin_keys[0].reshape(block_rows, q_heads, HEAD_SIZE).transpose(1, 0, 2)
    cumulative = jnp.cumsum(decay_logs[0], axis=1)
    lower_mask = jnp.arange(block_rows)[:, None] >= jnp.arange(block_rows)[None, :]
    gaps = jnp.where(lower_mask[None], cumulative[:, :, None] - cumulative[:, None, :], 0.0)
    products = jnp.einsum(
        "hsd,htd->hst", membrane_queries, membrane_keys, preferred_element_type=jnp.float32
    )
    decayed = jnp.where(lower_mask[None], jnp.exp(gaps), 0.0) * products
    spike_float = spikes.astype(jnp.float32)
    query_float = membrane_queries.astype(jnp.float32)
    key_float = membrane_keys.astype(jnp.float32)
    block_decay = jnp.exp(cumulative[:, -1])
    tail_decay = jnp.exp(cumulative[:, -1:] - cumulative)
    head_decay = jnp.exp(cumulative)
    local_state = jnp.einsum(
        "hsd,hse->hde", key_float * tail_decay[..., None], spike_float, precision=precise
    )
    incoming = (
        cotangent[0].reshape(block_rows, q_heads, HEAD_SIZE).transpose(1, 0, 2).astype(jnp.float32)
    )

    splits = min(HEAD_SPLITS, q_heads)
    bounds = [q_heads * part // splits for part in range(splits + 1)]
    unit_parts, grad_parts, gain_parts = [], [], []
    for low, high in zip(bounds[:-1], bounds[1:]):
        part = slice(low, high)
        state_in = entering(block_decay[part], local_state[part], "seq", False)
        carried = jnp.einsum("hsd,hde->hse", query_float[part], state_in, precision=precise)
        membrane = (
            jnp.einsum("hst,htd->hsd", decayed[part], spike_float[part], precision=precise)
            + head_decay[part][..., None] * carried
        )
        scale_out = 1.0 / jnp.sqrt(jnp.mean(membrane * membrane, axis=-1) + epsilon)
        unit_out = membrane * scale_out[..., None]
        membrane_grad = scale_out[..., None] * (
            incoming[part] - unit_out * jnp.mean(incoming[part] * unit_out, axis=-1, keepdims=True)
        )
        head_part = jnp.einsum(
            "hsd,hse->hde",
            query_float[part] * head_decay[part][..., None],
            membrane_grad,
            precision=precise,
        )
        state_after = entering(block_decay[part], head_part, "seq", True)
        later_part = jnp.einsum("htd,hde->hte", key_float[part], state_after, precision=precise)
        spike_grad = (
            jnp.einsum("hst,hsd->htd", decayed[part], membrane_grad, precision=precise)
            + tail_decay[part][..., None] * later_part
        )
        part_level = spike_grad * (1.0 - bounded[part] * bounded[part])
        part_gain = jnp.sum(part_level * normed[part], axis=1).reshape((high - low) * HEAD_SIZE)
        gain_parts.append(part_gain)
        unit_parts.append(unit_out)
        grad_parts.append(part_level)
    unit_out = jnp.concatenate(unit_parts, axis=0)
    level_grad = jnp.concatenate(grad_parts, axis=0)
    gain_grads = summed(jnp.concatenate(gain_parts, axis=0), ("seq", "dp"))
    layer_output = (
        unit_out.astype(jnp.bfloat16).transpose(1, 0, 2).reshape(1, block_rows, q_heads * HEAD_SIZE)
    )
    normed_grad = level_grad * gain_rows
    slope_sum = summed(jnp.sum(normed_grad * normed, axis=(0, 2)), ("tensor",))
    output_gradient = (
        inverse[None, :, None] * (normed_grad - normed * (slope_sum / D)[None, :, None])
    ).astype(jnp.bfloat16)

    grad_rows = output_gradient.reshape(kv_heads, head_groups, block_rows, HEAD_SIZE)
    prob_grad = jnp.einsum(
        "gjsd,gkd->gjsk", grad_rows, window_values, preferred_element_type=jnp.float32
    )
    row_delta = jnp.sum(probs * prob_grad, axis=-1, keepdims=True)
    logit_grad = (probs * (prob_grad - row_delta) * scaling).astype(jnp.bfloat16)
    query_parts = jnp.einsum(
        "gjsk,gkd->gjsd", logit_grad, window_keys, preferred_element_type=jnp.float32
    ).reshape(q_heads, block_rows, HEAD_SIZE)
    key_sum = jnp.einsum(
        "gjsk,gjsd->gkd", logit_grad, group_queries, preferred_element_type=jnp.float32
    )
    value_sum = jnp.einsum(
        "gjsk,gjsd->gkd", weights, grad_rows, preferred_element_type=jnp.float32
    )
    pair_grads = jnp.stack([key_sum, value_sum])
    total_grads = pair_grads[:, :, key_span:]
    for distance in range(previous, 0, -1):
        offset = (previous - distance) * block_rows
        total_grads = total_grads + passed_along(
            pair_grads[:, :, offset : offset + block_rows], "seq", -distance
        )
    query_grads = (
        query_parts.astype(jnp.bfloat16)
        .transpose(1, 0, 2)
        .reshape(1, block_rows, q_heads * HEAD_SIZE)
    )
    key_gradient = (
        total_grads[0]
        .astype(jnp.bfloat16)
        .transpose(1, 0, 2)
        .reshape(1, block_rows, kv_heads * HEAD_SIZE)
    )
    value_gradient = (
        total_grads[1]
        .astype(jnp.bfloat16)
        .transpose(1, 0, 2)
        .reshape(1, block_rows, kv_heads * HEAD_SIZE)
    )
    return (layer_output, query_grads, key_gradient, value_gradient, gain_grads)


def solution(mesh):
    placed = (
        P("dp", "seq", "tensor"),
        P("dp", "seq", "tensor"),
        P("dp", "seq", "tensor"),
        P("tensor"),
        P("tensor"),
        P("tensor"),
        P("dp", "seq", "tensor"),
        P("dp", "seq", "tensor"),
        P("dp", "tensor", "seq"),
        P("dp", "seq", "tensor"),
    )
    return jax.shard_map(
        local,
        mesh=mesh,
        in_specs=placed,
        out_specs=(
            P("dp", "seq", "tensor"),
            P("dp", "seq", "tensor"),
            P("dp", "seq", "tensor"),
            P("dp", "seq", "tensor"),
            P("tensor"),
        ),
        check_vma=False,
    )
```

```python
import math

import jax
import jax.numpy as jnp
from jax import lax
from jax.sharding import PartitionSpec as P

HEAD_SIZE = 128
D = 3584
LONGEST_WINDOW = 512
HEAD_SPLITS = 1


precise = lax.Precision.HIGHEST
epsilon = 1e-06


def passed_along(block, axis, distance):
    devices = range(lax.axis_size(axis))
    route = [(i - distance, i) for i in devices if i - distance in devices]
    return lax.ppermute(block, axis, route)


def chain_states(earlier, later):
    rows = later.shape[1] - 8
    is_state = jnp.arange(later.shape[1])[None, :, None] < rows
    return jnp.where(is_state, later[:, rows : rows + 1, :1] * earlier + later, earlier * later)


def picked(flag, new, old):
    return jnp.where(flag, new, old)


def moved_on(value, axis, pairs):
    return lax.ppermute(value, axis, pairs)


def entering(decay, state, axis, backward):
    count, index = (lax.axis_size(axis), lax.axis_index(axis))
    place = count - 1 - index if backward else index
    spot = (lambda p: count - 1 - p) if backward else (lambda p: p)
    rows = state.shape[1]
    value = jnp.concatenate(
        [state, jnp.broadcast_to(decay[:, None, None], (state.shape[0], 8, state.shape[2]))], axis=1
    )
    identity = jnp.concatenate([jnp.zeros_like(state), jnp.ones_like(value[:, rows:])], axis=1)
    if count % 2:
        before, covered, distance = identity, value, 1
        while distance < count:
            moved = moved_on(
                covered, axis, [(spot(p), spot(p + distance)) for p in range(count - distance)]
            )
            present = place >= distance
            before = picked(present, chain_states(moved, before), before)
            covered = picked(present, chain_states(moved, covered), covered)
            distance *= 2
        return before[:, :rows]
    lead = place % 2 == 1
    first = moved_on(value, axis, [(spot(p), spot(p + 1)) for p in range(0, count, 2)])
    covered = chain_states(first, value)
    before = identity
    distance = 2
    while distance < count:
        sent = covered.astype(jnp.bfloat16) if distance >= 4 else covered
        moved = moved_on(
            sent,
            axis,
            [(spot(p), spot(p + distance)) for p in range(1, count - distance, 2)],
        ).astype(jnp.float32)
        present = place >= distance
        before = picked(present, chain_states(moved, before), before)
        if 2 * distance < count:
            covered = picked(present, chain_states(moved, covered), covered)
        distance *= 2
    handed = moved_on(before[:, :rows], axis, [(spot(p), spot(p - 1)) for p in range(1, count, 2)])
    own_lead = chain_states(before, first)[:, :rows]
    return jnp.where(lead, own_lead, handed)


def xor_reduced(value, axis, offsets):
    count = lax.axis_size(axis)
    combos = [0]
    for offset in offsets:
        combos = combos + [c ^ offset for c in combos]
    values = {0: value}
    for c in combos[1:]:
        values[c] = lax.ppermute(value, axis, [(i, i ^ c) for i in range(count)])
    for offset in offsets:
        values = {c: values[c] + values[c ^ offset] for c in values if not c & offset}
    return values[0]


def summed(value, axes):
    for axis in axes:
        count = lax.axis_size(axis)
        if count & (count - 1):
            value = lax.psum(value, axis)
            continue
        for k in range(count.bit_length() - 1):
            value = xor_reduced(value, axis, [1 << k])
    return value


def local(
    attention_queries,
    attention_keys,
    attention_values,
    key_window_length,
    norm_gain,
    spike_levels,
    lin_queries,
    lin_keys,
    decay_logs,
    cotangent,
):
    block_rows = attention_queries.shape[1]
    q_heads = attention_queries.shape[2] // HEAD_SIZE
    kv_heads = attention_keys.shape[2] // HEAD_SIZE
    head_groups = q_heads // kv_heads
    previous = (LONGEST_WINDOW + block_rows - 1) // block_rows
    key_span = previous * block_rows
    window = key_span + block_rows
    first_query = lax.axis_index("seq") * block_rows
    scaling = 1.0 / math.sqrt(HEAD_SIZE)
    own_pair = jnp.stack([attention_keys, attention_values])
    earlier_blocks = [passed_along(own_pair, "seq", distance) for distance in range(previous, 0, -1)]
    window_pair = jnp.concatenate(earlier_blocks + [own_pair], axis=2)
    window_pair = window_pair.reshape(2, window, kv_heads, HEAD_SIZE).transpose(0, 2, 1, 3)
    window_keys = window_pair[0]
    window_values = window_pair[1]
    head_queries = attention_queries[0].reshape(block_rows, q_heads, HEAD_SIZE).transpose(1, 0, 2)
    group_queries = head_queries.reshape(kv_heads, head_groups, block_rows, HEAD_SIZE)

    query_pos = first_query + jnp.arange(block_rows, dtype=jnp.int32)[:, None]
    key_pos = first_query - key_span + jnp.arange(window, dtype=jnp.int32)[None, :]
    reach = key_window_length[:, None, None, None]
    allowed = (
        (key_pos >= 0)[None, None]
        & (key_pos <= query_pos)[None, None]
        & (key_pos[None, None] > query_pos[None, None] - reach)
    )
    logits = (
        jnp.einsum(
            "gjsd,gkd->gjsk", group_queries, window_keys, preferred_element_type=jnp.float32
        )
        * scaling
    )
    logits = jnp.where(allowed, logits, -jnp.inf)
    row_max = jnp.max(logits, axis=-1, keepdims=True)
    exponent = jnp.exp(logits - row_max)
    row_sum = jnp.sum(exponent, axis=-1, keepdims=True)
    probs = exponent / row_sum
    weights = probs.astype(jnp.bfloat16)
    heads_out = (
        jnp.einsum("gjsk,gkd->gjsd", weights, window_values, preferred_element_type=jnp.float32)
        .astype(jnp.bfloat16)
        .reshape(q_heads, block_rows, HEAD_SIZE)
    )

    out_float = heads_out.astype(jnp.float32)
    square_sum = summed(jnp.sum(out_float * out_float, axis=(0, 2)), ("tensor",))
    inverse = 1.0 / jnp.sqrt(square_sum / D + epsilon)
    normed = out_float * inverse[None, :, None]
    gain_rows = norm_gain.reshape(q_heads, HEAD_SIZE)[:, None, :]
    ceiling = spike_levels.astype(jnp.float32).reshape(q_heads, HEAD_SIZE)[:, None, :]
    bounded = jnp.tanh(normed * gain_rows / ceiling)
    spikes = (ceiling * bounded).astype(jnp.bfloat16)
    membrane_queries = lin_queries[0].reshape(block_rows, q_heads, HEAD_SIZE).transpose(1, 0, 2)
    membrane_keys = lin_keys[0].reshape(block_rows, q_heads, HEAD_SIZE).transpose(1, 0, 2)
    cumulative = jnp.cumsum(decay_logs[0], axis=1)
    lower_mask = jnp.arange(block_rows)[:, None] >= jnp.arange(block_rows)[None, :]
    gaps = jnp.where(lower_mask[None], cumulative[:, :, None] - cumulative[:, None, :], 0.0)
    products = jnp.einsum(
        "hsd,htd->hst", membrane_queries, membrane_keys, preferred_element_type=jnp.float32
    )
    decayed = jnp.where(lower_mask[None], jnp.exp(gaps), 0.0) * products
    spike_float = spikes.astype(jnp.float32)
    query_float = membrane_queries.astype(jnp.float32)
    key_float = membrane_keys.astype(jnp.float32)
    block_decay = jnp.exp(cumulative[:, -1])
    tail_decay = jnp.exp(cumulative[:, -1:] - cumulative)
    head_decay = jnp.exp(cumulative)
    local_state = jnp.einsum(
        "hsd,hse->hde", key_float * tail_decay[..., None], spike_float, precision=precise
    )
    incoming = (
        cotangent[0].reshape(block_rows, q_heads, HEAD_SIZE).transpose(1, 0, 2).astype(jnp.float32)
    )

    splits = min(HEAD_SPLITS, q_heads)
    bounds = [q_heads * part // splits for part in range(splits + 1)]
    unit_parts, grad_parts, gain_parts = [], [], []
    for low, high in zip(bounds[:-1], bounds[1:]):
        part = slice(low, high)
        state_in = entering(block_decay[part], local_state[part], "seq", False)
        carried = jnp.einsum("hsd,hde->hse", query_float[part], state_in, precision=precise)
        membrane = (
            jnp.einsum("hst,htd->hsd", decayed[part], spike_float[part], precision=precise)
            + head_decay[part][..., None] * carried
        )
        scale_out = 1.0 / jnp.sqrt(jnp.mean(membrane * membrane, axis=-1) + epsilon)
        unit_out = membrane * scale_out[..., None]
        membrane_grad = scale_out[..., None] * (
            incoming[part] - unit_out * jnp.mean(incoming[part] * unit_out, axis=-1, keepdims=True)
        )
        head_part = jnp.einsum(
            "hsd,hse->hde",
            query_float[part] * head_decay[part][..., None],
            membrane_grad,
            precision=precise,
        )
        state_after = entering(block_decay[part], head_part, "seq", True)
        later_part = jnp.einsum("htd,hde->hte", key_float[part], state_after, precision=precise)
        spike_grad = (
            jnp.einsum("hst,hsd->htd", decayed[part], membrane_grad, precision=precise)
            + tail_decay[part][..., None] * later_part
        )
        part_level = spike_grad * (1.0 - bounded[part] * bounded[part])
        part_gain = jnp.sum(part_level * normed[part], axis=1).reshape((high - low) * HEAD_SIZE)
        gain_parts.append(part_gain)
        unit_parts.append(unit_out)
        grad_parts.append(part_level)
    unit_out = jnp.concatenate(unit_parts, axis=0)
    level_grad = jnp.concatenate(grad_parts, axis=0)
    gain_grads = summed(jnp.concatenate(gain_parts, axis=0), ("seq", "dp"))
    layer_output = (
        unit_out.astype(jnp.bfloat16).transpose(1, 0, 2).reshape(1, block_rows, q_heads * HEAD_SIZE)
    )
    normed_grad = level_grad * gain_rows
    slope_sum = summed(jnp.sum(normed_grad * normed, axis=(0, 2)), ("tensor",))
    output_gradient = (
        inverse[None, :, None] * (normed_grad - normed * (slope_sum / D)[None, :, None])
    ).astype(jnp.bfloat16)

    grad_rows = output_gradient.reshape(kv_heads, head_groups, block_rows, HEAD_SIZE)
    prob_grad = jnp.einsum(
        "gjsd,gkd->gjsk", grad_rows, window_values, preferred_element_type=jnp.float32
    )
    row_delta = jnp.sum(probs * prob_grad, axis=-1, keepdims=True)
    logit_grad = (probs * (prob_grad - row_delta) * scaling).astype(jnp.bfloat16)
    query_parts = jnp.einsum(
        "gjsk,gkd->gjsd", logit_grad, window_keys, preferred_element_type=jnp.float32
    ).reshape(q_heads, block_rows, HEAD_SIZE)
    key_sum = jnp.einsum(
        "gjsk,gjsd->gkd", logit_grad, group_queries, preferred_element_type=jnp.float32
    )
    value_sum = jnp.einsum(
        "gjsk,gjsd->gkd", weights, grad_rows, preferred_element_type=jnp.float32
    )
    pair_grads = jnp.stack([key_sum, value_sum])
    total_grads = pair_grads[:, :, key_span:]
    for distance in range(previous, 0, -1):
        offset = (previous - distance) * block_rows
        total_grads = total_grads + passed_along(
            pair_grads[:, :, offset : offset + block_rows], "seq", -distance
        )
    query_grads = (
        query_parts.astype(jnp.bfloat16)
        .transpose(1, 0, 2)
        .reshape(1, block_rows, q_heads * HEAD_SIZE)
    )
    key_gradient = (
        total_grads[0]
        .astype(jnp.bfloat16)
        .transpose(1, 0, 2)
        .reshape(1, block_rows, kv_heads * HEAD_SIZE)
    )
    value_gradient = (
        total_grads[1]
        .astype(jnp.bfloat16)
        .transpose(1, 0, 2)
        .reshape(1, block_rows, kv_heads * HEAD_SIZE)
    )
    return (layer_output, query_grads, key_gradient, value_gradient, gain_grads)


def solution(mesh):
    placed = (
        P("dp", "seq", "tensor"),
        P("dp", "seq", "tensor"),
        P("dp", "seq", "tensor"),
        P("tensor"),
        P("tensor"),
        P("tensor"),
        P("dp", "seq", "tensor"),
        P("dp", "seq", "tensor"),
        P("dp", "tensor", "seq"),
        P("dp", "seq", "tensor"),
    )
    return jax.shard_map(
        local,
        mesh=mesh,
        in_specs=placed,
        out_specs=(
            P("dp", "seq", "tensor"),
            P("dp", "seq", "tensor"),
            P("dp", "seq", "tensor"),
            P("dp", "seq", "tensor"),
            P("tensor"),
        ),
        check_vma=False,
    )
```

```python
import math

import jax
import jax.numpy as jnp
from jax import lax
from jax.sharding import PartitionSpec as P

HEAD_SIZE = 128
D = 3584
LONGEST_WINDOW = 512
HEAD_SPLITS = 1


precise = lax.Precision.HIGHEST
epsilon = 1e-06


def passed_along(block, axis, distance):
    devices = range(lax.axis_size(axis))
    route = [(i - distance, i) for i in devices if i - distance in devices]
    return lax.ppermute(block, axis, route)


def chain_states(earlier, later):
    rows = later.shape[1] - 8
    is_state = jnp.arange(later.shape[1])[None, :, None] < rows
    return jnp.where(is_state, later[:, rows : rows + 1, :1] * earlier + later, earlier * later)


def picked(flag, new, old):
    return jnp.where(flag, new, old)


def moved_on(value, axis, pairs):
    return lax.ppermute(value, axis, pairs)


def entering(decay, state, axis, backward):
    count, index = (lax.axis_size(axis), lax.axis_index(axis))
    place = count - 1 - index if backward else index
    spot = (lambda p: count - 1 - p) if backward else (lambda p: p)
    rows = state.shape[1]
    value = jnp.concatenate(
        [state, jnp.broadcast_to(decay[:, None, None], (state.shape[0], 8, state.shape[2]))], axis=1
    )
    identity = jnp.concatenate([jnp.zeros_like(state), jnp.ones_like(value[:, rows:])], axis=1)
    if count % 2:
        before, covered, distance = identity, value, 1
        while distance < count:
            moved = moved_on(
                covered, axis, [(spot(p), spot(p + distance)) for p in range(count - distance)]
            )
            present = place >= distance
            before = picked(present, chain_states(moved, before), before)
            covered = picked(present, chain_states(moved, covered), covered)
            distance *= 2
        return before[:, :rows]
    lead = place % 2 == 1
    first = moved_on(value, axis, [(spot(p), spot(p + 1)) for p in range(0, count, 2)])
    covered = chain_states(first, value)
    before = identity
    distance = 2
    while distance < count:
        sent = covered.astype(jnp.bfloat16) if distance >= 4 else covered
        moved = moved_on(
            sent,
            axis,
            [(spot(p), spot(p + distance)) for p in range(1, count - distance, 2)],
        ).astype(jnp.float32)
        present = place >= distance
        before = picked(present, chain_states(moved, before), before)
        if 2 * distance < count:
            covered = picked(present, chain_states(moved, covered), covered)
        distance *= 2
    handed = moved_on(before[:, :rows], axis, [(spot(p), spot(p - 1)) for p in range(1, count, 2)])
    own_lead = chain_states(before, first)[:, :rows]
    return jnp.where(lead, own_lead, handed)


def xor_reduced(value, axis, offsets):
    count = lax.axis_size(axis)
    combos = [0]
    for offset in offsets:
        combos = combos + [c ^ offset for c in combos]
    values = {0: value}
    for c in combos[1:]:
        values[c] = lax.ppermute(value, axis, [(i, i ^ c) for i in range(count)])
    for offset in offsets:
        values = {c: values[c] + values[c ^ offset] for c in values if not c & offset}
    return values[0]


def summed(value, axes):
    for axis in axes:
        count = lax.axis_size(axis)
        if count & (count - 1):
            value = lax.psum(value, axis)
            continue
        for k in range(count.bit_length() - 1):
            value = xor_reduced(value, axis, [1 << k])
    return value


def local(
    attention_queries,
    attention_keys,
    attention_values,
    key_window_length,
    norm_gain,
    spike_levels,
    lin_queries,
    lin_keys,
    decay_logs,
    cotangent,
):
    block_rows = attention_queries.shape[1]
    q_heads = attention_queries.shape[2] // HEAD_SIZE
    kv_heads = attention_keys.shape[2] // HEAD_SIZE
    head_groups = q_heads // kv_heads
    previous = (LONGEST_WINDOW + block_rows - 1) // block_rows
    key_span = previous * block_rows
    window = key_span + block_rows
    first_query = lax.axis_index("seq") * block_rows
    scaling = 1.0 / math.sqrt(HEAD_SIZE)
    own_pair = jnp.stack([attention_keys, attention_values])
    earlier_blocks = [passed_along(own_pair, "seq", distance) for distance in range(previous, 0, -1)]
    window_pair = jnp.concatenate(earlier_blocks + [own_pair], axis=2)
    window_pair = window_pair.reshape(2, window, kv_heads, HEAD_SIZE).transpose(0, 2, 1, 3)
    window_keys = window_pair[0]
    window_values = window_pair[1]
    head_queries = attention_queries[0].reshape(block_rows, q_heads, HEAD_SIZE).transpose(1, 0, 2)
    group_queries = head_queries.reshape(kv_heads, head_groups, block_rows, HEAD_SIZE)

    query_pos = first_query + jnp.arange(block_rows, dtype=jnp.int32)[:, None]
    key_pos = first_query - key_span + jnp.arange(window, dtype=jnp.int32)[None, :]
    reach = key_window_length[:, None, None, None]
    allowed = (
        (key_pos >= 0)[None, None]
        & (key_pos <= query_pos)[None, None]
        & (key_pos[None, None] > query_pos[None, None] - reach)
    )
    logits = (
        jnp.einsum(
            "gjsd,gkd->gjsk", group_queries, window_keys, preferred_element_type=jnp.float32
        )
        * scaling
    )
    logits = jnp.where(allowed, logits, -jnp.inf)
    row_max = jnp.max(logits, axis=-1, keepdims=True)
    exponent = jnp.exp(logits - row_max)
    row_sum = jnp.sum(exponent, axis=-1, keepdims=True)
    probs = exponent / row_sum
    weights = probs.astype(jnp.bfloat16)
    heads_out = (
        jnp.einsum("gjsk,gkd->gjsd", weights, window_values, preferred_element_type=jnp.float32)
        .astype(jnp.bfloat16)
        .reshape(q_heads, block_rows, HEAD_SIZE)
    )

    out_float = heads_out.astype(jnp.float32)
    square_sum = summed(jnp.sum(out_float * out_float, axis=(0, 2)), ("tensor",))
    inverse = 1.0 / jnp.sqrt(square_sum / D + epsilon)
    normed = out_float * inverse[None, :, None]
    gain_rows = norm_gain.reshape(q_heads, HEAD_SIZE)[:, None, :]
    ceiling = spike_levels.astype(jnp.float32).reshape(q_heads, HEAD_SIZE)[:, None, :]
    bounded = jnp.tanh(normed * gain_rows / ceiling)
    spikes = (ceiling * bounded).astype(jnp.bfloat16)
    membrane_queries = lin_queries[0].reshape(block_rows, q_heads, HEAD_SIZE).transpose(1, 0, 2)
    membrane_keys = lin_keys[0].reshape(block_rows, q_heads, HEAD_SIZE).transpose(1, 0, 2)
    cumulative = jnp.cumsum(decay_logs[0], axis=1)
    lower_mask = jnp.arange(block_rows)[:, None] >= jnp.arange(block_rows)[None, :]
    gaps = jnp.where(lower_mask[None], cumulative[:, :, None] - cumulative[:, None, :], 0.0)
    products = jnp.einsum(
        "hsd,htd->hst", membrane_queries, membrane_keys, preferred_element_type=jnp.float32
    )
    decayed = jnp.where(lower_mask[None], jnp.exp(gaps), 0.0) * products
    spike_float = spikes.astype(jnp.float32)
    query_float = membrane_queries.astype(jnp.float32)
    key_float = membrane_keys.astype(jnp.float32)
    block_decay = jnp.exp(cumulative[:, -1])
    tail_decay = jnp.exp(cumulative[:, -1:] - cumulative)
    head_decay = jnp.exp(cumulative)
    local_state = jnp.einsum(
        "hsd,hse->hde", key_float * tail_decay[..., None], spike_float, precision=precise
    )
    incoming = (
        cotangent[0].reshape(block_rows, q_heads, HEAD_SIZE).transpose(1, 0, 2).astype(jnp.float32)
    )

    splits = min(HEAD_SPLITS, q_heads)
    bounds = [q_heads * part // splits for part in range(splits + 1)]
    unit_parts, grad_parts, gain_parts = [], [], []
    for low, high in zip(bounds[:-1], bounds[1:]):
        part = slice(low, high)
        state_in = entering(block_decay[part], local_state[part], "seq", False)
        carried = jnp.einsum("hsd,hde->hse", query_float[part], state_in, precision=precise)
        membrane = (
            jnp.einsum("hst,htd->hsd", decayed[part], spike_float[part], precision=precise)
            + head_decay[part][..., None] * carried
        )
        scale_out = 1.0 / jnp.sqrt(jnp.mean(membrane * membrane, axis=-1) + epsilon)
        unit_out = membrane * scale_out[..., None]
        membrane_grad = scale_out[..., None] * (
            incoming[part] - unit_out * jnp.mean(incoming[part] * unit_out, axis=-1, keepdims=True)
        )
        head_part = jnp.einsum(
            "hsd,hse->hde",
            query_float[part] * head_decay[part][..., None],
            membrane_grad,
            precision=precise,
        )
        state_after = entering(block_decay[part], head_part, "seq", True)
        later_part = jnp.einsum("htd,hde->hte", key_float[part], state_after, precision=precise)
        spike_grad = (
            jnp.einsum("hst,hsd->htd", decayed[part], membrane_grad, precision=precise)
            + tail_decay[part][..., None] * later_part
        )
        part_level = spike_grad * (1.0 - bounded[part] * bounded[part])
        part_gain = jnp.sum(part_level * normed[part], axis=1).reshape((high - low) * HEAD_SIZE)
        gain_parts.append(part_gain)
        unit_parts.append(unit_out)
        grad_parts.append(part_level)
    unit_out = jnp.concatenate(unit_parts, axis=0)
    level_grad = jnp.concatenate(grad_parts, axis=0)
    layer_output = (
        unit_out.astype(jnp.bfloat16).transpose(1, 0, 2).reshape(1, block_rows, q_heads * HEAD_SIZE)
    )
    normed_grad = level_grad * gain_rows
    slope_sum = summed(jnp.sum(normed_grad * normed, axis=(0, 2)), ("tensor",))
    output_gradient = (
        inverse[None, :, None] * (normed_grad - normed * (slope_sum / D)[None, :, None])
    ).astype(jnp.bfloat16)

    grad_rows = output_gradient.reshape(kv_heads, head_groups, block_rows, HEAD_SIZE)
    prob_grad = jnp.einsum(
        "gjsd,gkd->gjsk", grad_rows, window_values, preferred_element_type=jnp.float32
    )
    row_delta = jnp.sum(probs * prob_grad, axis=-1, keepdims=True)
    logit_grad = (probs * (prob_grad - row_delta) * scaling).astype(jnp.bfloat16)
    query_parts = jnp.einsum(
        "gjsk,gkd->gjsd", logit_grad, window_keys, preferred_element_type=jnp.float32
    ).reshape(q_heads, block_rows, HEAD_SIZE)
    key_sum = jnp.einsum(
        "gjsk,gjsd->gkd", logit_grad, group_queries, preferred_element_type=jnp.float32
    )
    value_sum = jnp.einsum(
        "gjsk,gjsd->gkd", weights, grad_rows, preferred_element_type=jnp.float32
    )
    pair_grads = jnp.stack([key_sum, value_sum])
    gain_part, pair_grads = lax.optimization_barrier((jnp.concatenate(gain_parts, axis=0), pair_grads))
    gain_grads = summed(gain_part, ("seq", "dp"))
    total_grads = pair_grads[:, :, key_span:]
    for distance in range(previous, 0, -1):
        offset = (previous - distance) * block_rows
        total_grads = total_grads + passed_along(
            pair_grads[:, :, offset : offset + block_rows], "seq", -distance
        )
    query_grads = (
        query_parts.astype(jnp.bfloat16)
        .transpose(1, 0, 2)
        .reshape(1, block_rows, q_heads * HEAD_SIZE)
    )
    key_gradient = (
        total_grads[0]
        .astype(jnp.bfloat16)
        .transpose(1, 0, 2)
        .reshape(1, block_rows, kv_heads * HEAD_SIZE)
    )
    value_gradient = (
        total_grads[1]
        .astype(jnp.bfloat16)
        .transpose(1, 0, 2)
        .reshape(1, block_rows, kv_heads * HEAD_SIZE)
    )
    return (layer_output, query_grads, key_gradient, value_gradient, gain_grads)


def solution(mesh):
    placed = (
        P("dp", "seq", "tensor"),
        P("dp", "seq", "tensor"),
        P("dp", "seq", "tensor"),
        P("tensor"),
        P("tensor"),
        P("tensor"),
        P("dp", "seq", "tensor"),
        P("dp", "seq", "tensor"),
        P("dp", "tensor", "seq"),
        P("dp", "seq", "tensor"),
    )
    return jax.shard_map(
        local,
        mesh=mesh,
        in_specs=placed,
        out_specs=(
            P("dp", "seq", "tensor"),
            P("dp", "seq", "tensor"),
            P("dp", "seq", "tensor"),
            P("dp", "seq", "tensor"),
            P("tensor"),
        ),
        check_vma=False,
    )
```

```python
import math

import jax
import jax.numpy as jnp
from jax import lax
from jax.sharding import PartitionSpec as P

HEAD_SIZE = 128
D = 3584
LONGEST_WINDOW = 512
HEAD_SPLITS = 1


precise = lax.Precision.HIGHEST
epsilon = 1e-06


def passed_along(block, axis, distance):
    devices = range(lax.axis_size(axis))
    route = [(i - distance, i) for i in devices if i - distance in devices]
    return lax.ppermute(block, axis, route)


def chain_states(earlier, later):
    rows = later.shape[1] - 8
    is_state = jnp.arange(later.shape[1])[None, :, None] < rows
    return jnp.where(is_state, later[:, rows : rows + 1, :1] * earlier + later, earlier * later)


def picked(flag, new, old):
    return jnp.where(flag, new, old)


def moved_on(value, axis, pairs):
    return lax.ppermute(value, axis, pairs)


def entering(decay, state, axis, backward):
    count, index = (lax.axis_size(axis), lax.axis_index(axis))
    place = count - 1 - index if backward else index
    spot = (lambda p: count - 1 - p) if backward else (lambda p: p)
    rows = state.shape[1]
    value = jnp.concatenate(
        [state, jnp.broadcast_to(decay[:, None, None], (state.shape[0], 8, state.shape[2]))], axis=1
    )
    identity = jnp.concatenate([jnp.zeros_like(state), jnp.ones_like(value[:, rows:])], axis=1)
    if count % 2:
        before, covered, distance = identity, value, 1
        while distance < count:
            moved = moved_on(
                covered, axis, [(spot(p), spot(p + distance)) for p in range(count - distance)]
            )
            present = place >= distance
            before = picked(present, chain_states(moved, before), before)
            covered = picked(present, chain_states(moved, covered), covered)
            distance *= 2
        return before[:, :rows]
    lead = place % 2 == 1
    first = moved_on(value, axis, [(spot(p), spot(p + 1)) for p in range(0, count, 2)])
    covered = chain_states(first, value)
    before = identity
    distance = 2
    while distance < count:
        sent = covered.astype(jnp.bfloat16)
        moved = moved_on(
            sent,
            axis,
            [(spot(p), spot(p + distance)) for p in range(1, count - distance, 2)],
        ).astype(jnp.float32)
        present = place >= distance
        before = picked(present, chain_states(moved, before), before)
        if 2 * distance < count:
            covered = picked(present, chain_states(moved, covered), covered)
        distance *= 2
    handed = moved_on(before[:, :rows], axis, [(spot(p), spot(p - 1)) for p in range(1, count, 2)])
    own_lead = chain_states(before, first)[:, :rows]
    return jnp.where(lead, own_lead, handed)


def xor_reduced(value, axis, offsets):
    count = lax.axis_size(axis)
    combos = [0]
    for offset in offsets:
        combos = combos + [c ^ offset for c in combos]
    values = {0: value}
    for c in combos[1:]:
        values[c] = lax.ppermute(value, axis, [(i, i ^ c) for i in range(count)])
    for offset in offsets:
        values = {c: values[c] + values[c ^ offset] for c in values if not c & offset}
    return values[0]


def summed(value, axes):
    for axis in axes:
        count = lax.axis_size(axis)
        if count & (count - 1):
            value = lax.psum(value, axis)
            continue
        for k in range(count.bit_length() - 1):
            value = xor_reduced(value, axis, [1 << k])
    return value


def local(
    attention_queries,
    attention_keys,
    attention_values,
    key_window_length,
    norm_gain,
    spike_levels,
    lin_queries,
    lin_keys,
    decay_logs,
    cotangent,
):
    block_rows = attention_queries.shape[1]
    q_heads = attention_queries.shape[2] // HEAD_SIZE
    kv_heads = attention_keys.shape[2] // HEAD_SIZE
    head_groups = q_heads // kv_heads
    previous = (LONGEST_WINDOW + block_rows - 1) // block_rows
    key_span = previous * block_rows
    window = key_span + block_rows
    first_query = lax.axis_index("seq") * block_rows
    scaling = 1.0 / math.sqrt(HEAD_SIZE)
    own_pair = jnp.stack([attention_keys, attention_values])
    earlier_blocks = [passed_along(own_pair, "seq", distance) for distance in range(previous, 0, -1)]
    window_pair = jnp.concatenate(earlier_blocks + [own_pair], axis=2)
    window_pair = window_pair.reshape(2, window, kv_heads, HEAD_SIZE).transpose(0, 2, 1, 3)
    window_keys = window_pair[0]
    window_values = window_pair[1]
    head_queries = attention_queries[0].reshape(block_rows, q_heads, HEAD_SIZE).transpose(1, 0, 2)
    group_queries = head_queries.reshape(kv_heads, head_groups, block_rows, HEAD_SIZE)

    query_pos = first_query + jnp.arange(block_rows, dtype=jnp.int32)[:, None]
    key_pos = first_query - key_span + jnp.arange(window, dtype=jnp.int32)[None, :]
    reach = key_window_length[:, None, None, None]
    allowed = (
        (key_pos >= 0)[None, None]
        & (key_pos <= query_pos)[None, None]
        & (key_pos[None, None] > query_pos[None, None] - reach)
    )
    logits = (
        jnp.einsum(
            "gjsd,gkd->gjsk", group_queries, window_keys, preferred_element_type=jnp.float32
        )
        * scaling
    )
    logits = jnp.where(allowed, logits, -jnp.inf)
    row_max = jnp.max(logits, axis=-1, keepdims=True)
    exponent = jnp.exp(logits - row_max)
    row_sum = jnp.sum(exponent, axis=-1, keepdims=True)
    probs = exponent / row_sum
    weights = probs.astype(jnp.bfloat16)
    heads_out = (
        jnp.einsum("gjsk,gkd->gjsd", weights, window_values, preferred_element_type=jnp.float32)
        .astype(jnp.bfloat16)
        .reshape(q_heads, block_rows, HEAD_SIZE)
    )

    out_float = heads_out.astype(jnp.float32)
    square_sum = lax.psum(jnp.sum(out_float * out_float, axis=(0, 2)), "tensor")
    inverse = 1.0 / jnp.sqrt(square_sum / D + epsilon)
    normed = out_float * inverse[None, :, None]
    gain_rows = norm_gain.reshape(q_heads, HEAD_SIZE)[:, None, :]
    ceiling = spike_levels.astype(jnp.float32).reshape(q_heads, HEAD_SIZE)[:, None, :]
    bounded = jnp.tanh(normed * gain_rows / ceiling)
    spikes = (ceiling * bounded).astype(jnp.bfloat16)
    membrane_queries = lin_queries[0].reshape(block_rows, q_heads, HEAD_SIZE).transpose(1, 0, 2)
    membrane_keys = lin_keys[0].reshape(block_rows, q_heads, HEAD_SIZE).transpose(1, 0, 2)
    cumulative = jnp.cumsum(decay_logs[0], axis=1)
    lower_mask = jnp.arange(block_rows)[:, None] >= jnp.arange(block_rows)[None, :]
    gaps = jnp.where(lower_mask[None], cumulative[:, :, None] - cumulative[:, None, :], 0.0)
    products = jnp.einsum(
        "hsd,htd->hst", membrane_queries, membrane_keys, preferred_element_type=jnp.float32
    )
    decayed = jnp.where(lower_mask[None], jnp.exp(gaps), 0.0) * products
    spike_float = spikes.astype(jnp.float32)
    query_float = membrane_queries.astype(jnp.float32)
    key_float = membrane_keys.astype(jnp.float32)
    block_decay = jnp.exp(cumulative[:, -1])
    tail_decay = jnp.exp(cumulative[:, -1:] - cumulative)
    head_decay = jnp.exp(cumulative)
    local_state = jnp.einsum(
        "hsd,hse->hde", key_float * tail_decay[..., None], spike_float, precision=precise
    )
    incoming = (
        cotangent[0].reshape(block_rows, q_heads, HEAD_SIZE).transpose(1, 0, 2).astype(jnp.float32)
    )

    splits = min(HEAD_SPLITS, q_heads)
    bounds = [q_heads * part // splits for part in range(splits + 1)]
    unit_parts, grad_parts, gain_parts = [], [], []
    for low, high in zip(bounds[:-1], bounds[1:]):
        part = slice(low, high)
        state_in = entering(block_decay[part], local_state[part], "seq", False)
        carried = jnp.einsum("hsd,hde->hse", query_float[part], state_in, precision=precise)
        membrane = (
            jnp.einsum("hst,htd->hsd", decayed[part], spike_float[part], precision=precise)
            + head_decay[part][..., None] * carried
        )
        scale_out = 1.0 / jnp.sqrt(jnp.mean(membrane * membrane, axis=-1) + epsilon)
        unit_out = membrane * scale_out[..., None]
        membrane_grad = scale_out[..., None] * (
            incoming[part] - unit_out * jnp.mean(incoming[part] * unit_out, axis=-1, keepdims=True)
        )
        head_part = jnp.einsum(
            "hsd,hse->hde",
            query_float[part] * head_decay[part][..., None],
            membrane_grad,
            precision=precise,
        )
        state_after = entering(block_decay[part], head_part, "seq", True)
        later_part = jnp.einsum("htd,hde->hte", key_float[part], state_after, precision=precise)
        spike_grad = (
            jnp.einsum("hst,hsd->htd", decayed[part], membrane_grad, precision=precise)
            + tail_decay[part][..., None] * later_part
        )
        part_level = spike_grad * (1.0 - bounded[part] * bounded[part])
        part_gain = jnp.sum(part_level * normed[part], axis=1).reshape((high - low) * HEAD_SIZE)
        gain_parts.append(part_gain)
        unit_parts.append(unit_out)
        grad_parts.append(part_level)
    unit_out = jnp.concatenate(unit_parts, axis=0)
    level_grad = jnp.concatenate(grad_parts, axis=0)
    gain_grads = summed(jnp.concatenate(gain_parts, axis=0), ("seq", "dp"))
    layer_output = (
        unit_out.astype(jnp.bfloat16).transpose(1, 0, 2).reshape(1, block_rows, q_heads * HEAD_SIZE)
    )
    normed_grad = level_grad * gain_rows
    slope_sum = lax.psum(jnp.sum(normed_grad * normed, axis=(0, 2)), "tensor")
    output_gradient = (
        inverse[None, :, None] * (normed_grad - normed * (slope_sum / D)[None, :, None])
    ).astype(jnp.bfloat16)

    grad_rows = output_gradient.reshape(kv_heads, head_groups, block_rows, HEAD_SIZE)
    prob_grad = jnp.einsum(
        "gjsd,gkd->gjsk", grad_rows, window_values, preferred_element_type=jnp.float32
    )
    row_delta = jnp.sum(probs * prob_grad, axis=-1, keepdims=True)
    logit_grad = (probs * (prob_grad - row_delta) * scaling).astype(jnp.bfloat16)
    query_parts = jnp.einsum(
        "gjsk,gkd->gjsd", logit_grad, window_keys, preferred_element_type=jnp.float32
    ).reshape(q_heads, block_rows, HEAD_SIZE)
    key_sum = jnp.einsum(
        "gjsk,gjsd->gkd", logit_grad, group_queries, preferred_element_type=jnp.float32
    )
    value_sum = jnp.einsum(
        "gjsk,gjsd->gkd", weights, grad_rows, preferred_element_type=jnp.float32
    )
    pair_grads = jnp.stack([key_sum, value_sum])
    total_grads = pair_grads[:, :, key_span:]
    for distance in range(previous, 0, -1):
        offset = (previous - distance) * block_rows
        total_grads = total_grads + passed_along(
            pair_grads[:, :, offset : offset + block_rows], "seq", -distance
        )
    query_grads = (
        query_parts.astype(jnp.bfloat16)
        .transpose(1, 0, 2)
        .reshape(1, block_rows, q_heads * HEAD_SIZE)
    )
    key_gradient = (
        total_grads[0]
        .astype(jnp.bfloat16)
        .transpose(1, 0, 2)
        .reshape(1, block_rows, kv_heads * HEAD_SIZE)
    )
    value_gradient = (
        total_grads[1]
        .astype(jnp.bfloat16)
        .transpose(1, 0, 2)
        .reshape(1, block_rows, kv_heads * HEAD_SIZE)
    )
    return (layer_output, query_grads, key_gradient, value_gradient, gain_grads)


def solution(mesh):
    placed = (
        P("dp", "seq", "tensor"),
        P("dp", "seq", "tensor"),
        P("dp", "seq", "tensor"),
        P("tensor"),
        P("tensor"),
        P("tensor"),
        P("dp", "seq", "tensor"),
        P("dp", "seq", "tensor"),
        P("dp", "tensor", "seq"),
        P("dp", "seq", "tensor"),
    )
    return jax.shard_map(
        local,
        mesh=mesh,
        in_specs=placed,
        out_specs=(
            P("dp", "seq", "tensor"),
            P("dp", "seq", "tensor"),
            P("dp", "seq", "tensor"),
            P("dp", "seq", "tensor"),
            P("tensor"),
        ),
        check_vma=False,
    )
```

```python
import math

import jax
import jax.numpy as jnp
from jax import lax
from jax.sharding import PartitionSpec as P

HEAD_SIZE = 128
D = 3584
LONGEST_WINDOW = 512
HEAD_SPLITS = 1


precise = lax.Precision.HIGHEST
epsilon = 1e-06


def passed_along(block, axis, distance):
    devices = range(lax.axis_size(axis))
    route = [(i - distance, i) for i in devices if i - distance in devices]
    return lax.ppermute(block, axis, route)


def chain_states(earlier, later):
    rows = later.shape[1] - 8
    is_state = jnp.arange(later.shape[1])[None, :, None] < rows
    return jnp.where(is_state, later[:, rows : rows + 1, :1] * earlier + later, earlier * later)


def picked(flag, new, old):
    return jnp.where(flag, new, old)


def moved_on(value, axis, pairs):
    return lax.ppermute(value, axis, pairs)


def entering(decay, state, axis, backward):
    count, index = (lax.axis_size(axis), lax.axis_index(axis))
    place = count - 1 - index if backward else index
    spot = (lambda p: count - 1 - p) if backward else (lambda p: p)
    rows = state.shape[1]
    value = jnp.concatenate(
        [state, jnp.broadcast_to(decay[:, None, None], (state.shape[0], 8, state.shape[2]))], axis=1
    )
    identity = jnp.concatenate([jnp.zeros_like(state), jnp.ones_like(value[:, rows:])], axis=1)
    if count % 2:
        before, covered, distance = identity, value, 1
        while distance < count:
            moved = moved_on(
                covered, axis, [(spot(p), spot(p + distance)) for p in range(count - distance)]
            )
            present = place >= distance
            before = picked(present, chain_states(moved, before), before)
            covered = picked(present, chain_states(moved, covered), covered)
            distance *= 2
        return before[:, :rows]
    lead = place % 2 == 1
    first = moved_on(value, axis, [(spot(p), spot(p + 1)) for p in range(0, count, 2)])
    covered = chain_states(first, value)
    before = identity
    distance = 2
    while distance < count:
        sent = covered.astype(jnp.bfloat16)
        moved = moved_on(
            sent,
            axis,
            [(spot(p), spot(p + distance)) for p in range(1, count - distance, 2)],
        ).astype(jnp.float32)
        present = place >= distance
        before = picked(present, chain_states(moved, before), before)
        if 2 * distance < count:
            covered = picked(present, chain_states(moved, covered), covered)
        distance *= 2
    handed = moved_on(before[:, :rows], axis, [(spot(p), spot(p - 1)) for p in range(1, count, 2)])
    own_lead = chain_states(before, first)[:, :rows]
    return jnp.where(lead, own_lead, handed)


def xor_reduced(value, axis, offsets):
    count = lax.axis_size(axis)
    combos = [0]
    for offset in offsets:
        combos = combos + [c ^ offset for c in combos]
    values = {0: value}
    for c in combos[1:]:
        values[c] = lax.ppermute(value, axis, [(i, i ^ c) for i in range(count)])
    for offset in offsets:
        values = {c: values[c] + values[c ^ offset] for c in values if not c & offset}
    return values[0]


def summed(value, axes):
    for axis in axes:
        count = lax.axis_size(axis)
        if count & (count - 1):
            value = lax.psum(value, axis)
            continue
        for k in range(count.bit_length() - 1):
            value = xor_reduced(value, axis, [1 << k])
    return value


def local(
    attention_queries,
    attention_keys,
    attention_values,
    key_window_length,
    norm_gain,
    spike_levels,
    lin_queries,
    lin_keys,
    decay_logs,
    cotangent,
):
    block_rows = attention_queries.shape[1]
    q_heads = attention_queries.shape[2] // HEAD_SIZE
    kv_heads = attention_keys.shape[2] // HEAD_SIZE
    head_groups = q_heads // kv_heads
    previous = (LONGEST_WINDOW + block_rows - 1) // block_rows
    key_span = previous * block_rows
    window = key_span + block_rows
    first_query = lax.axis_index("seq") * block_rows
    scaling = 1.0 / math.sqrt(HEAD_SIZE)
    own_pair = jnp.stack([attention_keys, attention_values])
    earlier_blocks = [passed_along(own_pair, "seq", distance) for distance in range(previous, 0, -1)]
    window_pair = jnp.concatenate(earlier_blocks + [own_pair], axis=2)
    window_pair = window_pair.reshape(2, window, kv_heads, HEAD_SIZE).transpose(0, 2, 1, 3)
    window_keys = window_pair[0]
    window_values = window_pair[1]
    head_queries = attention_queries[0].reshape(block_rows, q_heads, HEAD_SIZE).transpose(1, 0, 2)
    group_queries = head_queries.reshape(kv_heads, head_groups, block_rows, HEAD_SIZE)

    query_pos = first_query + jnp.arange(block_rows, dtype=jnp.int32)[:, None]
    key_pos = first_query - key_span + jnp.arange(window, dtype=jnp.int32)[None, :]
    reach = key_window_length[:, None, None, None]
    allowed = (
        (key_pos >= 0)[None, None]
        & (key_pos <= query_pos)[None, None]
        & (key_pos[None, None] > query_pos[None, None] - reach)
    )
    logits = (
        jnp.einsum(
            "gjsd,gkd->gjsk", group_queries, window_keys, preferred_element_type=jnp.float32
        )
        * scaling
    )
    logits = jnp.where(allowed, logits, -jnp.inf)
    row_max = jnp.max(logits, axis=-1, keepdims=True)
    exponent = jnp.exp(logits - row_max)
    row_sum = jnp.sum(exponent, axis=-1, keepdims=True)
    probs = exponent / row_sum
    weights = probs.astype(jnp.bfloat16)
    heads_out = (
        jnp.einsum("gjsk,gkd->gjsd", weights, window_values, preferred_element_type=jnp.float32)
        .astype(jnp.bfloat16)
        .reshape(q_heads, block_rows, HEAD_SIZE)
    )

    out_float = heads_out.astype(jnp.float32)
    square_sum = lax.psum(jnp.sum(out_float * out_float, axis=(0, 2)), "tensor")
    inverse = 1.0 / jnp.sqrt(square_sum / D + epsilon)
    normed = out_float * inverse[None, :, None]
    gain_rows = norm_gain.reshape(q_heads, HEAD_SIZE)[:, None, :]
    ceiling = spike_levels.astype(jnp.float32).reshape(q_heads, HEAD_SIZE)[:, None, :]
    bounded = jnp.tanh(normed * gain_rows / ceiling)
    spikes = (ceiling * bounded).astype(jnp.bfloat16)
    membrane_queries = lin_queries[0].reshape(block_rows, q_heads, HEAD_SIZE).transpose(1, 0, 2)
    membrane_keys = lin_keys[0].reshape(block_rows, q_heads, HEAD_SIZE).transpose(1, 0, 2)
    cumulative = jnp.cumsum(decay_logs[0], axis=1)
    lower_mask = jnp.arange(block_rows)[:, None] >= jnp.arange(block_rows)[None, :]
    gaps = jnp.where(lower_mask[None], cumulative[:, :, None] - cumulative[:, None, :], 0.0)
    products = jnp.einsum(
        "hsd,htd->hst", membrane_queries, membrane_keys, preferred_element_type=jnp.float32
    )
    decayed = jnp.where(lower_mask[None], jnp.exp(gaps), 0.0) * products
    spike_float = spikes.astype(jnp.float32)
    query_float = membrane_queries.astype(jnp.float32)
    key_float = membrane_keys.astype(jnp.float32)
    block_decay = jnp.exp(cumulative[:, -1])
    tail_decay = jnp.exp(cumulative[:, -1:] - cumulative)
    head_decay = jnp.exp(cumulative)
    local_state = jnp.einsum(
        "hsd,hse->hde", key_float * tail_decay[..., None], spike_float, precision=precise
    )
    incoming = (
        cotangent[0].reshape(block_rows, q_heads, HEAD_SIZE).transpose(1, 0, 2).astype(jnp.float32)
    )

    splits = min(HEAD_SPLITS, q_heads)
    bounds = [q_heads * part // splits for part in range(splits + 1)]
    unit_parts, grad_parts, gain_parts = [], [], []
    for low, high in zip(bounds[:-1], bounds[1:]):
        part = slice(low, high)
        state_in = entering(block_decay[part], local_state[part], "seq", False)
        carried = jnp.einsum("hsd,hde->hse", query_float[part], state_in, precision=precise)
        membrane = (
            jnp.einsum("hst,htd->hsd", decayed[part], spike_float[part], precision=precise)
            + head_decay[part][..., None] * carried
        )
        scale_out = 1.0 / jnp.sqrt(jnp.mean(membrane * membrane, axis=-1) + epsilon)
        unit_out = membrane * scale_out[..., None]
        membrane_grad = scale_out[..., None] * (
            incoming[part] - unit_out * jnp.mean(incoming[part] * unit_out, axis=-1, keepdims=True)
        )
        head_part = jnp.einsum(
            "hsd,hse->hde",
            query_float[part] * head_decay[part][..., None],
            membrane_grad,
            precision=precise,
        )
        state_after = entering(block_decay[part], head_part, "seq", True)
        later_part = jnp.einsum("htd,hde->hte", key_float[part], state_after, precision=precise)
        spike_grad = (
            jnp.einsum("hst,hsd->htd", decayed[part], membrane_grad, precision=precise)
            + tail_decay[part][..., None] * later_part
        )
        part_level = spike_grad * (1.0 - bounded[part] * bounded[part])
        part_gain = jnp.sum(part_level * normed[part], axis=1).reshape((high - low) * HEAD_SIZE)
        gain_parts.append(part_gain)
        unit_parts.append(unit_out)
        grad_parts.append(part_level)
    unit_out = jnp.concatenate(unit_parts, axis=0)
    level_grad = jnp.concatenate(grad_parts, axis=0)
    gain_grads = lax.psum(summed(jnp.concatenate(gain_parts, axis=0), ("seq",)), "dp")
    layer_output = (
        unit_out.astype(jnp.bfloat16).transpose(1, 0, 2).reshape(1, block_rows, q_heads * HEAD_SIZE)
    )
    normed_grad = level_grad * gain_rows
    slope_sum = lax.psum(jnp.sum(normed_grad * normed, axis=(0, 2)), "tensor")
    output_gradient = (
        inverse[None, :, None] * (normed_grad - normed * (slope_sum / D)[None, :, None])
    ).astype(jnp.bfloat16)

    grad_rows = output_gradient.reshape(kv_heads, head_groups, block_rows, HEAD_SIZE)
    prob_grad = jnp.einsum(
        "gjsd,gkd->gjsk", grad_rows, window_values, preferred_element_type=jnp.float32
    )
    row_delta = jnp.sum(probs * prob_grad, axis=-1, keepdims=True)
    logit_grad = (probs * (prob_grad - row_delta) * scaling).astype(jnp.bfloat16)
    query_parts = jnp.einsum(
        "gjsk,gkd->gjsd", logit_grad, window_keys, preferred_element_type=jnp.float32
    ).reshape(q_heads, block_rows, HEAD_SIZE)
    key_sum = jnp.einsum(
        "gjsk,gjsd->gkd", logit_grad, group_queries, preferred_element_type=jnp.float32
    )
    value_sum = jnp.einsum(
        "gjsk,gjsd->gkd", weights, grad_rows, preferred_element_type=jnp.float32
    )
    pair_grads = jnp.stack([key_sum, value_sum])
    total_grads = pair_grads[:, :, key_span:]
    for distance in range(previous, 0, -1):
        offset = (previous - distance) * block_rows
        total_grads = total_grads + passed_along(
            pair_grads[:, :, offset : offset + block_rows], "seq", -distance
        )
    query_grads = (
        query_parts.astype(jnp.bfloat16)
        .transpose(1, 0, 2)
        .reshape(1, block_rows, q_heads * HEAD_SIZE)
    )
    key_gradient = (
        total_grads[0]
        .astype(jnp.bfloat16)
        .transpose(1, 0, 2)
        .reshape(1, block_rows, kv_heads * HEAD_SIZE)
    )
    value_gradient = (
        total_grads[1]
        .astype(jnp.bfloat16)
        .transpose(1, 0, 2)
        .reshape(1, block_rows, kv_heads * HEAD_SIZE)
    )
    return (layer_output, query_grads, key_gradient, value_gradient, gain_grads)


def solution(mesh):
    placed = (
        P("dp", "seq", "tensor"),
        P("dp", "seq", "tensor"),
        P("dp", "seq", "tensor"),
        P("tensor"),
        P("tensor"),
        P("tensor"),
        P("dp", "seq", "tensor"),
        P("dp", "seq", "tensor"),
        P("dp", "tensor", "seq"),
        P("dp", "seq", "tensor"),
    )
    return jax.shard_map(
        local,
        mesh=mesh,
        in_specs=placed,
        out_specs=(
            P("dp", "seq", "tensor"),
            P("dp", "seq", "tensor"),
            P("dp", "seq", "tensor"),
            P("dp", "seq", "tensor"),
            P("tensor"),
        ),
        check_vma=False,
    )
```

```python
import math

import jax
import jax.numpy as jnp
from jax import lax
from jax.sharding import PartitionSpec as P

HEAD_SIZE = 128
D = 3584
LONGEST_WINDOW = 512
HEAD_SPLITS = 1


precise = lax.Precision.HIGHEST
epsilon = 1e-06


def passed_along(block, axis, distance):
    devices = range(lax.axis_size(axis))
    route = [(i - distance, i) for i in devices if i - distance in devices]
    return lax.ppermute(block, axis, route)


def chain_states(earlier, later):
    rows = later.shape[1] - 8
    is_state = jnp.arange(later.shape[1])[None, :, None] < rows
    return jnp.where(is_state, later[:, rows : rows + 1, :1] * earlier + later, earlier * later)


def picked(flag, new, old):
    return jnp.where(flag, new, old)


def moved_on(value, axis, pairs):
    return lax.ppermute(value, axis, pairs)


def entering(decay, state, axis, backward):
    count, index = (lax.axis_size(axis), lax.axis_index(axis))
    place = count - 1 - index if backward else index
    spot = (lambda p: count - 1 - p) if backward else (lambda p: p)
    rows = state.shape[1]
    value = jnp.concatenate(
        [state, jnp.broadcast_to(decay[:, None, None], (state.shape[0], 8, state.shape[2]))], axis=1
    )
    identity = jnp.concatenate([jnp.zeros_like(state), jnp.ones_like(value[:, rows:])], axis=1)
    if count % 2:
        before, covered, distance = identity, value, 1
        while distance < count:
            moved = moved_on(
                covered, axis, [(spot(p), spot(p + distance)) for p in range(count - distance)]
            )
            present = place >= distance
            before = picked(present, chain_states(moved, before), before)
            covered = picked(present, chain_states(moved, covered), covered)
            distance *= 2
        return before[:, :rows]
    lead = place % 2 == 1
    first = moved_on(
        value.astype(jnp.bfloat16), axis, [(spot(p), spot(p + 1)) for p in range(0, count, 2)]
    ).astype(jnp.float32)
    covered = chain_states(first, value)
    before = identity
    distance = 2
    while distance < count:
        sent = covered.astype(jnp.bfloat16)
        moved = moved_on(
            sent,
            axis,
            [(spot(p), spot(p + distance)) for p in range(1, count - distance, 2)],
        ).astype(jnp.float32)
        present = place >= distance
        before = picked(present, chain_states(moved, before), before)
        if 2 * distance < count:
            covered = picked(present, chain_states(moved, covered), covered)
        distance *= 2
    handed = moved_on(
        before[:, :rows].astype(jnp.bfloat16), axis, [(spot(p), spot(p - 1)) for p in range(1, count, 2)]
    ).astype(jnp.float32)
    own_lead = chain_states(before, first)[:, :rows]
    return jnp.where(lead, own_lead, handed)


def xor_reduced(value, axis, offsets):
    count = lax.axis_size(axis)
    combos = [0]
    for offset in offsets:
        combos = combos + [c ^ offset for c in combos]
    values = {0: value}
    for c in combos[1:]:
        values[c] = lax.ppermute(value, axis, [(i, i ^ c) for i in range(count)])
    for offset in offsets:
        values = {c: values[c] + values[c ^ offset] for c in values if not c & offset}
    return values[0]


def summed(value, axes):
    for axis in axes:
        count = lax.axis_size(axis)
        if count & (count - 1):
            value = lax.psum(value, axis)
            continue
        for k in range(count.bit_length() - 1):
            value = xor_reduced(value, axis, [1 << k])
    return value


def local(
    attention_queries,
    attention_keys,
    attention_values,
    key_window_length,
    norm_gain,
    spike_levels,
    lin_queries,
    lin_keys,
    decay_logs,
    cotangent,
):
    block_rows = attention_queries.shape[1]
    q_heads = attention_queries.shape[2] // HEAD_SIZE
    kv_heads = attention_keys.shape[2] // HEAD_SIZE
    head_groups = q_heads // kv_heads
    previous = (LONGEST_WINDOW + block_rows - 1) // block_rows
    key_span = previous * block_rows
    window = key_span + block_rows
    first_query = lax.axis_index("seq") * block_rows
    scaling = 1.0 / math.sqrt(HEAD_SIZE)
    own_pair = jnp.stack([attention_keys, attention_values])
    earlier_blocks = [passed_along(own_pair, "seq", distance) for distance in range(previous, 0, -1)]
    window_pair = jnp.concatenate(earlier_blocks + [own_pair], axis=2)
    window_pair = window_pair.reshape(2, window, kv_heads, HEAD_SIZE).transpose(0, 2, 1, 3)
    window_keys = window_pair[0]
    window_values = window_pair[1]
    head_queries = attention_queries[0].reshape(block_rows, q_heads, HEAD_SIZE).transpose(1, 0, 2)
    group_queries = head_queries.reshape(kv_heads, head_groups, block_rows, HEAD_SIZE)

    query_pos = first_query + jnp.arange(block_rows, dtype=jnp.int32)[:, None]
    key_pos = first_query - key_span + jnp.arange(window, dtype=jnp.int32)[None, :]
    reach = key_window_length[:, None, None, None]
    allowed = (
        (key_pos >= 0)[None, None]
        & (key_pos <= query_pos)[None, None]
        & (key_pos[None, None] > query_pos[None, None] - reach)
    )
    logits = (
        jnp.einsum(
            "gjsd,gkd->gjsk", group_queries, window_keys, preferred_element_type=jnp.float32
        )
        * scaling
    )
    logits = jnp.where(allowed, logits, -jnp.inf)
    row_max = jnp.max(logits, axis=-1, keepdims=True)
    exponent = jnp.exp(logits - row_max)
    row_sum = jnp.sum(exponent, axis=-1, keepdims=True)
    probs = exponent / row_sum
    weights = probs.astype(jnp.bfloat16)
    heads_out = (
        jnp.einsum("gjsk,gkd->gjsd", weights, window_values, preferred_element_type=jnp.float32)
        .astype(jnp.bfloat16)
        .reshape(q_heads, block_rows, HEAD_SIZE)
    )

    out_float = heads_out.astype(jnp.float32)
    square_sum = lax.psum(jnp.sum(out_float * out_float, axis=(0, 2)), "tensor")
    inverse = 1.0 / jnp.sqrt(square_sum / D + epsilon)
    normed = out_float * inverse[None, :, None]
    gain_rows = norm_gain.reshape(q_heads, HEAD_SIZE)[:, None, :]
    ceiling = spike_levels.astype(jnp.float32).reshape(q_heads, HEAD_SIZE)[:, None, :]
    bounded = jnp.tanh(normed * gain_rows / ceiling)
    spikes = (ceiling * bounded).astype(jnp.bfloat16)
    membrane_queries = lin_queries[0].reshape(block_rows, q_heads, HEAD_SIZE).transpose(1, 0, 2)
    membrane_keys = lin_keys[0].reshape(block_rows, q_heads, HEAD_SIZE).transpose(1, 0, 2)
    cumulative = jnp.cumsum(decay_logs[0], axis=1)
    lower_mask = jnp.arange(block_rows)[:, None] >= jnp.arange(block_rows)[None, :]
    gaps = jnp.where(lower_mask[None], cumulative[:, :, None] - cumulative[:, None, :], 0.0)
    products = jnp.einsum(
        "hsd,htd->hst", membrane_queries, membrane_keys, preferred_element_type=jnp.float32
    )
    decayed = jnp.where(lower_mask[None], jnp.exp(gaps), 0.0) * products
    spike_float = spikes.astype(jnp.float32)
    query_float = membrane_queries.astype(jnp.float32)
    key_float = membrane_keys.astype(jnp.float32)
    block_decay = jnp.exp(cumulative[:, -1])
    tail_decay = jnp.exp(cumulative[:, -1:] - cumulative)
    head_decay = jnp.exp(cumulative)
    local_state = jnp.einsum(
        "hsd,hse->hde", key_float * tail_decay[..., None], spike_float, precision=precise
    )
    incoming = (
        cotangent[0].reshape(block_rows, q_heads, HEAD_SIZE).transpose(1, 0, 2).astype(jnp.float32)
    )

    splits = min(HEAD_SPLITS, q_heads)
    bounds = [q_heads * part // splits for part in range(splits + 1)]
    unit_parts, grad_parts, gain_parts = [], [], []
    for low, high in zip(bounds[:-1], bounds[1:]):
        part = slice(low, high)
        state_in = entering(block_decay[part], local_state[part], "seq", False)
        carried = jnp.einsum("hsd,hde->hse", query_float[part], state_in, precision=precise)
        membrane = (
            jnp.einsum("hst,htd->hsd", decayed[part], spike_float[part], precision=precise)
            + head_decay[part][..., None] * carried
        )
        scale_out = 1.0 / jnp.sqrt(jnp.mean(membrane * membrane, axis=-1) + epsilon)
        unit_out = membrane * scale_out[..., None]
        membrane_grad = scale_out[..., None] * (
            incoming[part] - unit_out * jnp.mean(incoming[part] * unit_out, axis=-1, keepdims=True)
        )
        head_part = jnp.einsum(
            "hsd,hse->hde",
            query_float[part] * head_decay[part][..., None],
            membrane_grad,
            precision=precise,
        )
        state_after = entering(block_decay[part], head_part, "seq", True)
        later_part = jnp.einsum("htd,hde->hte", key_float[part], state_after, precision=precise)
        spike_grad = (
            jnp.einsum("hst,hsd->htd", decayed[part], membrane_grad, precision=precise)
            + tail_decay[part][..., None] * later_part
        )
        part_level = spike_grad * (1.0 - bounded[part] * bounded[part])
        part_gain = jnp.sum(part_level * normed[part], axis=1).reshape((high - low) * HEAD_SIZE)
        gain_parts.append(part_gain)
        unit_parts.append(unit_out)
        grad_parts.append(part_level)
    unit_out = jnp.concatenate(unit_parts, axis=0)
    level_grad = jnp.concatenate(grad_parts, axis=0)
    gain_grads = lax.psum(summed(jnp.concatenate(gain_parts, axis=0), ("seq",)), "dp")
    layer_output = (
        unit_out.astype(jnp.bfloat16).transpose(1, 0, 2).reshape(1, block_rows, q_heads * HEAD_SIZE)
    )
    normed_grad = level_grad * gain_rows
    slope_sum = lax.psum(jnp.sum(normed_grad * normed, axis=(0, 2)), "tensor")
    output_gradient = (
        inverse[None, :, None] * (normed_grad - normed * (slope_sum / D)[None, :, None])
    ).astype(jnp.bfloat16)

    grad_rows = output_gradient.reshape(kv_heads, head_groups, block_rows, HEAD_SIZE)
    prob_grad = jnp.einsum(
        "gjsd,gkd->gjsk", grad_rows, window_values, preferred_element_type=jnp.float32
    )
    row_delta = jnp.sum(probs * prob_grad, axis=-1, keepdims=True)
    logit_grad = (probs * (prob_grad - row_delta) * scaling).astype(jnp.bfloat16)
    query_parts = jnp.einsum(
        "gjsk,gkd->gjsd", logit_grad, window_keys, preferred_element_type=jnp.float32
    ).reshape(q_heads, block_rows, HEAD_SIZE)
    key_sum = jnp.einsum(
        "gjsk,gjsd->gkd", logit_grad, group_queries, preferred_element_type=jnp.float32
    )
    value_sum = jnp.einsum(
        "gjsk,gjsd->gkd", weights, grad_rows, preferred_element_type=jnp.float32
    )
    pair_grads = jnp.stack([key_sum, value_sum])
    total_grads = pair_grads[:, :, key_span:]
    for distance in range(previous, 0, -1):
        offset = (previous - distance) * block_rows
        total_grads = total_grads + passed_along(
            pair_grads[:, :, offset : offset + block_rows], "seq", -distance
        )
    query_grads = (
        query_parts.astype(jnp.bfloat16)
        .transpose(1, 0, 2)
        .reshape(1, block_rows, q_heads * HEAD_SIZE)
    )
    key_gradient = (
        total_grads[0]
        .astype(jnp.bfloat16)
        .transpose(1, 0, 2)
        .reshape(1, block_rows, kv_heads * HEAD_SIZE)
    )
    value_gradient = (
        total_grads[1]
        .astype(jnp.bfloat16)
        .transpose(1, 0, 2)
        .reshape(1, block_rows, kv_heads * HEAD_SIZE)
    )
    return (layer_output, query_grads, key_gradient, value_gradient, gain_grads)


def solution(mesh):
    placed = (
        P("dp", "seq", "tensor"),
        P("dp", "seq", "tensor"),
        P("dp", "seq", "tensor"),
        P("tensor"),
        P("tensor"),
        P("tensor"),
        P("dp", "seq", "tensor"),
        P("dp", "seq", "tensor"),
        P("dp", "tensor", "seq"),
        P("dp", "seq", "tensor"),
    )
    return jax.shard_map(
        local,
        mesh=mesh,
        in_specs=placed,
        out_specs=(
            P("dp", "seq", "tensor"),
            P("dp", "seq", "tensor"),
            P("dp", "seq", "tensor"),
            P("dp", "seq", "tensor"),
            P("tensor"),
        ),
        check_vma=False,
    )
```

```python
import math

import jax
import jax.numpy as jnp
from jax import lax
from jax.sharding import PartitionSpec as P

HEAD_SIZE = 128
D = 3584
LONGEST_WINDOW = 512
HEAD_SPLITS = 1


precise = lax.Precision.HIGHEST
epsilon = 1e-06


def passed_along(block, axis, distance):
    devices = range(lax.axis_size(axis))
    route = [(i - distance, i) for i in devices if i - distance in devices]
    return lax.ppermute(block, axis, route)


def chain_states(earlier, later):
    rows = later.shape[1] - 8
    is_state = jnp.arange(later.shape[1])[None, :, None] < rows
    return jnp.where(is_state, later[:, rows : rows + 1, :1] * earlier + later, earlier * later)


def picked(flag, new, old):
    return jnp.where(flag, new, old)


def moved_on(value, axis, pairs):
    return lax.ppermute(value, axis, pairs)


def entering(decay, state, axis, backward):
    count, index = (lax.axis_size(axis), lax.axis_index(axis))
    place = count - 1 - index if backward else index
    spot = (lambda p: count - 1 - p) if backward else (lambda p: p)
    rows = state.shape[1]
    value = jnp.concatenate(
        [state, jnp.broadcast_to(decay[:, None, None], (state.shape[0], 8, state.shape[2]))], axis=1
    )
    identity = jnp.concatenate([jnp.zeros_like(state), jnp.ones_like(value[:, rows:])], axis=1)
    if count % 2:
        before, covered, distance = identity, value, 1
        while distance < count:
            moved = moved_on(
                covered, axis, [(spot(p), spot(p + distance)) for p in range(count - distance)]
            )
            present = place >= distance
            before = picked(present, chain_states(moved, before), before)
            covered = picked(present, chain_states(moved, covered), covered)
            distance *= 2
        return before[:, :rows]
    lead = place % 2 == 1
    first = moved_on(
        value.astype(jnp.bfloat16), axis, [(spot(p), spot(p + 1)) for p in range(0, count, 2)]
    ).astype(jnp.float32)
    covered = chain_states(first, value)
    before = identity
    distance = 2
    while distance < count:
        sent = covered.astype(jnp.bfloat16)
        moved = moved_on(
            sent,
            axis,
            [(spot(p), spot(p + distance)) for p in range(1, count - distance, 2)],
        ).astype(jnp.float32)
        present = place >= distance
        before = picked(present, chain_states(moved, before), before)
        if 2 * distance < count:
            covered = picked(present, chain_states(moved, covered), covered)
        distance *= 2
    handed = moved_on(
        before[:, :rows].astype(jnp.bfloat16), axis, [(spot(p), spot(p - 1)) for p in range(1, count, 2)]
    ).astype(jnp.float32)
    own_lead = chain_states(before, first)[:, :rows]
    return jnp.where(lead, own_lead, handed)


def xor_reduced(value, axis, offsets):
    count = lax.axis_size(axis)
    combos = [0]
    for offset in offsets:
        combos = combos + [c ^ offset for c in combos]
    values = {0: value}
    for c in combos[1:]:
        values[c] = lax.ppermute(value, axis, [(i, i ^ c) for i in range(count)])
    for offset in offsets:
        values = {c: values[c] + values[c ^ offset] for c in values if not c & offset}
    return values[0]


def summed(value, axes):
    for axis in axes:
        count = lax.axis_size(axis)
        if count & (count - 1):
            value = lax.psum(value, axis)
            continue
        for k in range(count.bit_length() - 1):
            value = xor_reduced(value, axis, [1 << k])
    return value


def local(
    attention_queries,
    attention_keys,
    attention_values,
    key_window_length,
    norm_gain,
    spike_levels,
    lin_queries,
    lin_keys,
    decay_logs,
    cotangent,
):
    block_rows = attention_queries.shape[1]
    q_heads = attention_queries.shape[2] // HEAD_SIZE
    kv_heads = attention_keys.shape[2] // HEAD_SIZE
    head_groups = q_heads // kv_heads
    previous = (LONGEST_WINDOW + block_rows - 1) // block_rows
    key_span = previous * block_rows
    window = key_span + block_rows
    first_query = lax.axis_index("seq") * block_rows
    scaling = 1.0 / math.sqrt(HEAD_SIZE)
    own_pair = jnp.stack([attention_keys, attention_values])
    earlier_blocks = [passed_along(own_pair, "seq", distance) for distance in range(previous, 0, -1)]
    window_pair = jnp.concatenate(earlier_blocks + [own_pair], axis=2)
    window_pair = window_pair.reshape(2, window, kv_heads, HEAD_SIZE).transpose(0, 2, 1, 3)
    window_keys = window_pair[0]
    window_values = window_pair[1]
    head_queries = attention_queries[0].reshape(block_rows, q_heads, HEAD_SIZE).transpose(1, 0, 2)
    group_queries = head_queries.reshape(kv_heads, head_groups, block_rows, HEAD_SIZE)

    query_pos = first_query + jnp.arange(block_rows, dtype=jnp.int32)[:, None]
    key_pos = first_query - key_span + jnp.arange(window, dtype=jnp.int32)[None, :]
    reach = key_window_length[:, None, None, None]
    allowed = (
        (key_pos >= 0)[None, None]
        & (key_pos <= query_pos)[None, None]
        & (key_pos[None, None] > query_pos[None, None] - reach)
    )
    logits = (
        jnp.einsum(
            "gjsd,gkd->gjsk", group_queries, window_keys, preferred_element_type=jnp.float32
        )
        * scaling
    )
    logits = jnp.where(allowed, logits, -jnp.inf)
    row_max = jnp.max(logits, axis=-1, keepdims=True)
    exponent = jnp.exp(logits - row_max)
    row_sum = jnp.sum(exponent, axis=-1, keepdims=True)
    probs = exponent / row_sum
    weights = probs.astype(jnp.bfloat16)
    heads_out = (
        jnp.einsum("gjsk,gkd->gjsd", weights, window_values, preferred_element_type=jnp.float32)
        .astype(jnp.bfloat16)
        .reshape(q_heads, block_rows, HEAD_SIZE)
    )

    out_float = heads_out.astype(jnp.float32)
    square_sum = lax.psum(jnp.sum(out_float * out_float, axis=(0, 2)), "tensor")
    inverse = 1.0 / jnp.sqrt(square_sum / D + epsilon)
    normed = out_float * inverse[None, :, None]
    gain_rows = norm_gain.reshape(q_heads, HEAD_SIZE)[:, None, :]
    ceiling = spike_levels.astype(jnp.float32).reshape(q_heads, HEAD_SIZE)[:, None, :]
    bounded = jnp.tanh(normed * gain_rows / ceiling)
    spikes = (ceiling * bounded).astype(jnp.bfloat16)
    membrane_queries = lin_queries[0].reshape(block_rows, q_heads, HEAD_SIZE).transpose(1, 0, 2)
    membrane_keys = lin_keys[0].reshape(block_rows, q_heads, HEAD_SIZE).transpose(1, 0, 2)
    cumulative = jnp.cumsum(decay_logs[0], axis=1)
    lower_mask = jnp.arange(block_rows)[:, None] >= jnp.arange(block_rows)[None, :]
    gaps = jnp.where(lower_mask[None], cumulative[:, :, None] - cumulative[:, None, :], 0.0)
    products = jnp.einsum(
        "hsd,htd->hst", membrane_queries, membrane_keys, preferred_element_type=jnp.float32
    )
    decayed = jnp.where(lower_mask[None], jnp.exp(gaps), 0.0) * products
    spike_float = spikes.astype(jnp.float32)
    query_float = membrane_queries.astype(jnp.float32)
    key_float = membrane_keys.astype(jnp.float32)
    block_decay = jnp.exp(cumulative[:, -1])
    tail_decay = jnp.exp(cumulative[:, -1:] - cumulative)
    head_decay = jnp.exp(cumulative)
    local_state = jnp.einsum(
        "hsd,hse->hde", key_float * tail_decay[..., None], spike_float, precision=precise
    )
    incoming = (
        cotangent[0].reshape(block_rows, q_heads, HEAD_SIZE).transpose(1, 0, 2).astype(jnp.float32)
    )

    splits = min(HEAD_SPLITS, q_heads)
    bounds = [q_heads * part // splits for part in range(splits + 1)]
    unit_parts, grad_parts, gain_parts = [], [], []
    for low, high in zip(bounds[:-1], bounds[1:]):
        part = slice(low, high)
        state_in = entering(block_decay[part], local_state[part], "seq", False)
        carried = jnp.einsum("hsd,hde->hse", query_float[part], state_in, precision=precise)
        membrane = (
            jnp.einsum("hst,htd->hsd", decayed[part], spike_float[part], precision=precise)
            + head_decay[part][..., None] * carried
        )
        scale_out = 1.0 / jnp.sqrt(jnp.mean(membrane * membrane, axis=-1) + epsilon)
        unit_out = membrane * scale_out[..., None]
        membrane_grad = scale_out[..., None] * (
            incoming[part] - unit_out * jnp.mean(incoming[part] * unit_out, axis=-1, keepdims=True)
        )
        head_part = jnp.einsum(
            "hsd,hse->hde",
            query_float[part] * head_decay[part][..., None],
            membrane_grad,
            precision=precise,
        )
        state_after = entering(block_decay[part], head_part, "seq", True)
        later_part = jnp.einsum("htd,hde->hte", key_float[part], state_after, precision=precise)
        spike_grad = (
            jnp.einsum("hst,hsd->htd", decayed[part], membrane_grad, precision=precise)
            + tail_decay[part][..., None] * later_part
        )
        part_level = spike_grad * (1.0 - bounded[part] * bounded[part])
        part_gain = jnp.sum(part_level * normed[part], axis=1).reshape((high - low) * HEAD_SIZE)
        gain_parts.append(part_gain)
        unit_parts.append(unit_out)
        grad_parts.append(part_level)
    unit_out = jnp.concatenate(unit_parts, axis=0)
    level_grad = jnp.concatenate(grad_parts, axis=0)
    gain_grads = lax.psum(lax.psum(jnp.concatenate(gain_parts, axis=0), "seq"), "dp")
    layer_output = (
        unit_out.astype(jnp.bfloat16).transpose(1, 0, 2).reshape(1, block_rows, q_heads * HEAD_SIZE)
    )
    normed_grad = level_grad * gain_rows
    slope_sum = lax.psum(jnp.sum(normed_grad * normed, axis=(0, 2)), "tensor")
    output_gradient = (
        inverse[None, :, None] * (normed_grad - normed * (slope_sum / D)[None, :, None])
    ).astype(jnp.bfloat16)

    grad_rows = output_gradient.reshape(kv_heads, head_groups, block_rows, HEAD_SIZE)
    prob_grad = jnp.einsum(
        "gjsd,gkd->gjsk", grad_rows, window_values, preferred_element_type=jnp.float32
    )
    row_delta = jnp.sum(probs * prob_grad, axis=-1, keepdims=True)
    logit_grad = (probs * (prob_grad - row_delta) * scaling).astype(jnp.bfloat16)
    query_parts = jnp.einsum(
        "gjsk,gkd->gjsd", logit_grad, window_keys, preferred_element_type=jnp.float32
    ).reshape(q_heads, block_rows, HEAD_SIZE)
    key_sum = jnp.einsum(
        "gjsk,gjsd->gkd", logit_grad, group_queries, preferred_element_type=jnp.float32
    )
    value_sum = jnp.einsum(
        "gjsk,gjsd->gkd", weights, grad_rows, preferred_element_type=jnp.float32
    )
    pair_grads = jnp.stack([key_sum, value_sum])
    total_grads = pair_grads[:, :, key_span:]
    for distance in range(previous, 0, -1):
        offset = (previous - distance) * block_rows
        total_grads = total_grads + passed_along(
            pair_grads[:, :, offset : offset + block_rows], "seq", -distance
        )
    query_grads = (
        query_parts.astype(jnp.bfloat16)
        .transpose(1, 0, 2)
        .reshape(1, block_rows, q_heads * HEAD_SIZE)
    )
    key_gradient = (
        total_grads[0]
        .astype(jnp.bfloat16)
        .transpose(1, 0, 2)
        .reshape(1, block_rows, kv_heads * HEAD_SIZE)
    )
    value_gradient = (
        total_grads[1]
        .astype(jnp.bfloat16)
        .transpose(1, 0, 2)
        .reshape(1, block_rows, kv_heads * HEAD_SIZE)
    )
    return (layer_output, query_grads, key_gradient, value_gradient, gain_grads)


def solution(mesh):
    placed = (
        P("dp", "seq", "tensor"),
        P("dp", "seq", "tensor"),
        P("dp", "seq", "tensor"),
        P("tensor"),
        P("tensor"),
        P("tensor"),
        P("dp", "seq", "tensor"),
        P("dp", "seq", "tensor"),
        P("dp", "tensor", "seq"),
        P("dp", "seq", "tensor"),
    )
    return jax.shard_map(
        local,
        mesh=mesh,
        in_specs=placed,
        out_specs=(
            P("dp", "seq", "tensor"),
            P("dp", "seq", "tensor"),
            P("dp", "seq", "tensor"),
            P("dp", "seq", "tensor"),
            P("tensor"),
        ),
        check_vma=False,
    )
```
